256 devices in a mesh: seq: 64 (over y_lo, x, z), chan: 4 (over y_hi, core).
Axes of the slice: x: 4, y: 4 (y_hi: 2, y_lo: 2; y = y_hi * 2 + y_lo), z: 8, core: 2. Of those that a mesh axis runs over, the one named last changes fastest.
Arguments:
- qkv: bfloat16 [3, 4096, 8192], P(None, 'chan', 'seq'), may hold values from -6 to 6
- taps: float32 [3, 3, 4096], P(None, None, 'chan'), may hold values from -3 to 3
- lifetimes: float32 [16, 4096], P(None, 'chan'), may hold values from 12 to 32768, as said below
- residues: float32 [16, 4096], P(None, 'chan'), may hold values from -1 to 1
- out_weight: bfloat16 [4096, 4096], P('chan'), may hold values from -0.09375 to 0.09375
Outputs:
- output: bfloat16 [4096, 8192], P('chan', 'seq')
The draws below stay inside these ranges and needn't reach their ends.
Inputs may be any that keep to these rules, and one draw needn't show every extreme that they name: `lifetimes`: of every channel.
All inputs are finite; a program needn't handle non-finite values.
Results may differ from the reference program's by a relative error of at most 0.012.
Values may be sent and summed in bfloat16 or wider, within the bound.
No kernel may reach another device: no remote copies, remote signals or barrier semaphores. Data moves between devices by JAX's collectives and lax.ppermute only.
A program may use at most 128 MiB of HBM per device.

```python
import math
import jax
import jax.numpy as jnp
from jax import lax

CH = 4096
DOUT = 4096
MODES = 16
TOKENS = 8192


def lifetime_values(key):
    uniform_draw = jax.random.uniform(jax.random.fold_in(key, 11), (MODES, CH), jnp.float32)
    log_low = math.log(12.0)
    log_high = math.log(4.0 * TOKENS)
    return jnp.exp(log_low + uniform_draw * (log_high - log_low))


def draw_lifetimes(key, part):
    return lifetime_values(key)


def draw_residues(key, part):
    life_values = lifetime_values(key)
    noise_draw = jax.random.truncated_normal(jax.random.fold_in(key, 13), -4.0, 4.0, (MODES, CH), jnp.float32)
    return noise_draw * jnp.sqrt(2.0 / (life_values * MODES))


def levels(key, shape, split, low, high):
    loudness = 1.0
    for axis_at, shards_of in split:
        draws = jax.random.uniform(jax.random.fold_in(jax.random.fold_in(key, 6), axis_at), (shards_of,), jnp.float32, low / len(split), high / len(split))
        loudness = loudness * jnp.repeat(jnp.exp(draws), shape[axis_at] // shards_of).reshape((-1,) + (1,) * (len(shape) - 1 - axis_at))
    return loudness


def bell_draw(rng, dims, width, bound, pieces=(), kind=jnp.bfloat16):
    values = width * jax.random.normal(rng, dims, jnp.float32)
    if pieces:
        values = values * levels(rng, dims, pieces, -0.22, 0.18)
    return jnp.clip(values, -bound, bound).astype(kind)


def setup_inputs(seed: int = 0) -> dict:
    key_list = jax.random.split(jax.random.key(seed), 6)
    return {
        "qkv": bell_draw(key_list[0], (3, CH, TOKENS), 1.0, 6.0, ((1, 4), (2, 64))),
        "taps": bell_draw(key_list[1], (3, 3, CH), 0.6, 3.0, ((2, 4),), jnp.float32),
        "lifetimes": draw_lifetimes(jax.random.fold_in(key_list[5], 71), 0),
        "residues": draw_residues(jax.random.fold_in(key_list[5], 71), 0),
        "out_weight": bell_draw(key_list[4], (CH, DOUT), CH ** -0.5, 0.09375, ((0, 4),)),
    }


def shifted(signal, offset):
    padding = jnp.zeros(signal.shape[:-1] + (offset,), signal.dtype)
    return jnp.concatenate([padding, signal[..., : signal.shape[-1] - offset]], axis=-1)


def channel_block(block_args):
    inputs, tap_block, life_block, resid_block = block_args
    signal = inputs.astype(jnp.float32)
    filtered = (tap_block[:, 0, :, None] * signal
                + tap_block[:, 1, :, None] * shifted(signal, 1)
                + tap_block[:, 2, :, None] * shifted(signal, 2))
    product = (filtered[1] * filtered[2]).astype(jnp.bfloat16)
    product = lax.optimization_barrier(product).astype(jnp.float32)
    length = signal.shape[-1]
    times = jnp.arange(length).astype(jnp.float32)
    kernel = jnp.zeros(product.shape, jnp.float32)
    for mode_index in range(MODES):
        kernel = kernel + resid_block[mode_index][:, None] * jnp.exp(-times[None, :] / life_block[mode_index][:, None])
    fft_size = 2 * length
    spectrum = jnp.fft.rfft(product, n=fft_size, axis=-1) * jnp.fft.rfft(kernel, n=fft_size, axis=-1)
    convolved = jnp.fft.irfft(spectrum, n=fft_size, axis=-1)[:, :length].astype(jnp.bfloat16)
    convolved = lax.optimization_barrier(convolved).astype(jnp.float32)
    return (filtered[0] * convolved).astype(jnp.bfloat16)


def reference(qkv, taps, lifetimes, residues, out_weight):
    blocks = CH // 256
    inputs = qkv.reshape(3, blocks, 256, TOKENS).transpose(1, 0, 2, 3)
    tap_blocks = taps.reshape(3, 3, blocks, 256).transpose(2, 0, 1, 3)
    life_blocks = lifetimes.reshape(MODES, blocks, 256).transpose(1, 0, 2)
    resid_blocks = residues.reshape(MODES, blocks, 256).transpose(1, 0, 2)
    gated_rows = lax.map(channel_block, (inputs, tap_blocks, life_blocks, resid_blocks))
    gated_rows = gated_rows.reshape(CH, TOKENS)
    output = jnp.dot(out_weight.T, gated_rows, preferred_element_type=jnp.float32)
    return output.astype(jnp.bfloat16)
```

```python
import jax
import jax.numpy as jnp
from jax import lax
from jax.sharding import PartitionSpec as P


def from_behind(x, axis, by):
    devices = lax.axis_size(axis)
    pairs = [(i, i + by) for i in range(devices) if 0 <= i + by < devices]
    return lax.ppermute(x, axis, pairs)


def chunk_conv(product, lifetimes, residues):
    chan_here, tok = product.shape
    inv = 1.0 / lifetimes
    mid = tok // 2
    offs = (jnp.arange(tok, dtype=jnp.int32) - mid).astype(jnp.float32)
    grow = jnp.exp(offs[None, None, :] * inv[:, :, None])
    weighted = grow * product[None]
    upper = (
        jnp.arange(tok, dtype=jnp.int32)[:, None] <= jnp.arange(tok, dtype=jnp.int32)[None, :]
    ).astype(jnp.float32)
    sums = jnp.dot(weighted, upper, precision=lax.Precision.HIGH)
    decay = jnp.exp(-offs[None, None, :] * inv[:, :, None])
    local_part = jnp.sum(residues[:, :, None] * decay * sums, axis=0)
    state = jnp.exp(-float(tok - 1 - mid) * inv) * sums[:, :, tok - 1]

    seq_n = lax.axis_size("seq")
    inclusive = state
    exclusive = jnp.zeros_like(state)
    dist = 1
    while dist < seq_n:
        got = from_behind(inclusive, "seq", dist)
        exclusive = exclusive + jnp.exp(-float(tok * (dist - 1)) * inv) * got
        if 2 * dist < seq_n:
            inclusive = inclusive + jnp.exp(-float(tok * dist) * inv) * got
        dist *= 2

    steps = (jnp.arange(tok, dtype=jnp.int32) + 1).astype(jnp.float32)
    carried = jnp.sum(
        (residues * exclusive)[:, :, None] * jnp.exp(-steps[None, None, :] * inv[:, :, None]),
        axis=0,
    )
    return local_part + carried


def local(qkv, taps, lifetimes, residues, out_weight):
    tok_count = qkv.shape[2]
    edge_block = qkv[:, :, tok_count - 2 :]
    earlier = from_behind(edge_block, "seq", 1)
    extended = jnp.concatenate([earlier, qkv], axis=2).astype(jnp.float32)
    filtered = (
        taps[:, 0, :, None] * extended[:, :, 2:]
        + taps[:, 1, :, None] * extended[:, :, 1:-1]
        + taps[:, 2, :, None] * extended[:, :, :-2]
    )
    product = (filtered[1] * filtered[2]).astype(jnp.bfloat16).astype(jnp.float32)
    convolved = chunk_conv(product, lifetimes, residues).astype(jnp.bfloat16)
    gated_rows = (filtered[0] * convolved.astype(jnp.float32)).astype(jnp.bfloat16)
    return lax.psum_scatter(
        lax.dot_general(
            out_weight, gated_rows, (((0,), (0,)), ((), ())), preferred_element_type=jnp.float32
        ).astype(jnp.bfloat16),
        "chan",
        scatter_dimension=0,
        tiled=True,
    )


def solution(mesh):
    placed = (
        P(None, "chan", "seq"),
        P(None, None, "chan"),
        P(None, "chan"),
        P(None, "chan"),
        P("chan", None),
    )
    return jax.shard_map(
        local, mesh=mesh, in_specs=placed, out_specs=P("chan", "seq"), check_vma=False
    )
```

```python
import jax
import jax.numpy as jnp
from jax import lax
from jax.sharding import PartitionSpec as P


def from_behind(x, axis, by):
    devices = lax.axis_size(axis)
    pairs = [(i, i + by) for i in range(devices) if 0 <= i + by < devices]
    return lax.ppermute(x, axis, pairs)


def modal_conv(pencils, life_slice, resid_slice, block=128):
    chan_here, length = pencils.shape
    blocks = length // block
    inv = 1.0 / life_slice
    mid = block // 2
    offs = (jnp.arange(block, dtype=jnp.int32) - mid).astype(jnp.float32)
    grow = jnp.exp(offs[None, None, :] * inv[:, :, None])
    shrink = jnp.exp(-offs[None, None, :] * inv[:, :, None])
    signal = pencils.astype(jnp.float32).reshape(chan_here, blocks, block)
    weighted = grow[:, :, None, :] * signal[None]
    upper = (
        jnp.arange(block, dtype=jnp.int32)[:, None] <= jnp.arange(block, dtype=jnp.int32)[None, :]
    ).astype(jnp.float32)
    sums = jnp.dot(weighted, upper, precision=lax.Precision.HIGH)
    leaving = jnp.exp(-float(block - 1 - mid) * inv)[:, :, None] * sums[..., block - 1]
    n_idx = jnp.arange(blocks, dtype=jnp.int32)
    gap = (n_idx[:, None] - 1 - n_idx[None, :]).astype(jnp.float32)
    exponent = jnp.where(
        (n_idx[:, None] > n_idx[None, :])[None, None],
        -float(block) * gap[None, None] * inv[:, :, None, None],
        -jnp.inf,
    )
    entering = jnp.sum(jnp.exp(exponent) * leaving[:, :, None, :], axis=-1)
    carry_in = jnp.exp(-float(mid + 1) * inv)[:, :, None] * entering
    total = sums + carry_in[..., None]
    result = jnp.sum((resid_slice[:, :, None] * shrink)[:, :, None, :] * total, axis=0)
    return result.reshape(chan_here, length)


def reduce_scatter_chan(partial):
    index = lax.axis_index("chan")
    chip, core = index // 2, index % 2
    quarters = partial.reshape(2, 2, partial.shape[0] // 4, partial.shape[1])
    send = lax.dynamic_index_in_dim(quarters, 1 - core, 1, keepdims=False)
    keep = lax.dynamic_index_in_dim(quarters, core, 1, keepdims=False)
    got = lax.ppermute(send, "chan", [(j, j ^ 1) for j in range(4)])
    halves = keep.astype(jnp.float32) + got.astype(jnp.float32)
    send2 = lax.dynamic_index_in_dim(halves, 1 - chip, 0, keepdims=False).astype(jnp.bfloat16)
    keep2 = lax.dynamic_index_in_dim(halves, chip, 0, keepdims=False)
    got2 = lax.ppermute(send2, "chan", [(j, j ^ 2) for j in range(4)])
    return (keep2 + got2.astype(jnp.float32)).astype(jnp.bfloat16)


def local(qkv, taps, lifetimes, residues, out_weight):
    chan_local = qkv.shape[1]
    tok_count = qkv.shape[2]
    edge_block = qkv[:, :, tok_count - 2 :]
    earlier = from_behind(edge_block, "seq", 1)
    extended = jnp.concatenate([earlier, qkv], axis=2).astype(jnp.float32)
    filtered = (
        taps[:, 0, :, None] * extended[:, :, 2:]
        + taps[:, 1, :, None] * extended[:, :, 1:-1]
        + taps[:, 2, :, None] * extended[:, :, :-2]
    )
    product = (filtered[1] * filtered[2]).astype(jnp.bfloat16)
    groups = lax.axis_size("seq")
    per_group = chan_local // groups
    pencils = lax.all_to_all(product, "seq", split_axis=0, concat_axis=1, tiled=True)
    first_chan = lax.axis_index("seq") * per_group
    life_slice = lax.dynamic_slice_in_dim(lifetimes, first_chan, per_group, 1)
    resid_slice = lax.dynamic_slice_in_dim(residues, first_chan, per_group, 1)
    convolved = modal_conv(pencils, life_slice, resid_slice).astype(jnp.bfloat16)
    returned = lax.all_to_all(convolved, "seq", split_axis=1, concat_axis=0, tiled=True)
    gated_rows = (filtered[0] * returned.astype(jnp.float32)).astype(jnp.bfloat16)
    partial = lax.dot_general(
        out_weight, gated_rows, (((0,), (0,)), ((), ())), preferred_element_type=jnp.float32
    ).astype(jnp.bfloat16)
    return reduce_scatter_chan(partial)


def solution(mesh):
    placed = (
        P(None, "chan", "seq"),
        P(None, None, "chan"),
        P(None, "chan"),
        P(None, "chan"),
        P("chan", None),
    )
    return jax.shard_map(
        local, mesh=mesh, in_specs=placed, out_specs=P("chan", "seq"), check_vma=False
    )
```

```python
import jax
import jax.numpy as jnp
from jax import lax
from jax.sharding import PartitionSpec as P


def from_behind(x, axis, by):
    devices = lax.axis_size(axis)
    pairs = [(i, i + by) for i in range(devices) if 0 <= i + by < devices]
    return lax.ppermute(x, axis, pairs)


def modal_conv(pencils, life_slice, resid_slice, block=128):
    chan_here, length = pencils.shape
    blocks = length // block
    steps = jnp.arange(block, dtype=jnp.int32).astype(jnp.float32)
    life = life_slice[:, :, None]
    resid = resid_slice[:, :, None]
    taps = jnp.sum(resid * jnp.exp(-steps[None, None, :] / life), axis=0)
    lag = jnp.arange(block, dtype=jnp.int32)[None, :] - jnp.arange(block, dtype=jnp.int32)[:, None]
    toeplitz = jnp.where(lag[None] >= 0, jnp.take(taps, jnp.maximum(lag, 0), axis=1), 0.0)
    signal = pencils.astype(jnp.float32).reshape(chan_here, blocks, block)
    precise = lax.Precision.HIGH
    inside = jnp.einsum("cnj,cjt->cnt", signal, toeplitz, precision=precise)
    to_end = jnp.exp(-(float(block - 1) - steps)[None, None, :] / life)
    leaving = jnp.einsum("cnj,rcj->rcn", signal, to_end, precision=precise)
    n_idx = jnp.arange(blocks, dtype=jnp.int32)
    gap = (n_idx[:, None] - 1 - n_idx[None, :]).astype(jnp.float32)
    exponent = jnp.where(
        (n_idx[:, None] > n_idx[None, :])[None, None],
        -float(block) * gap[None, None] / life[..., None],
        -jnp.inf,
    )
    entering = jnp.sum(jnp.exp(exponent) * leaving[:, :, None, :], axis=-1)
    from_start = resid * jnp.exp(-(steps + 1.0)[None, None, :] / life)
    carried = jnp.einsum("rcn,rct->cnt", entering, from_start, precision=precise)
    return (inside + carried).reshape(chan_here, length)


def reduce_scatter_chan(partial):
    index = lax.axis_index("chan")
    chip, core = index // 2, index % 2
    quarters = partial.reshape(2, 2, partial.shape[0] // 4, partial.shape[1])
    send = lax.dynamic_index_in_dim(quarters, 1 - core, 1, keepdims=False)
    keep = lax.dynamic_index_in_dim(quarters, core, 1, keepdims=False)
    got = lax.ppermute(send, "chan", [(j, j ^ 1) for j in range(4)])
    halves = keep.astype(jnp.float32) + got.astype(jnp.float32)
    send2 = lax.dynamic_index_in_dim(halves, 1 - chip, 0, keepdims=False).astype(jnp.bfloat16)
    keep2 = lax.dynamic_index_in_dim(halves, chip, 0, keepdims=False)
    got2 = lax.ppermute(send2, "chan", [(j, j ^ 2) for j in range(4)])
    return (keep2 + got2.astype(jnp.float32)).astype(jnp.bfloat16)


def local(qkv, taps, lifetimes, residues, out_weight):
    chan_local = qkv.shape[1]
    tok_count = qkv.shape[2]
    edge_block = qkv[:, :, tok_count - 2 :]
    earlier = from_behind(edge_block, "seq", 1)
    extended = jnp.concatenate([earlier, qkv], axis=2).astype(jnp.float32)
    filtered = (
        taps[:, 0, :, None] * extended[:, :, 2:]
        + taps[:, 1, :, None] * extended[:, :, 1:-1]
        + taps[:, 2, :, None] * extended[:, :, :-2]
    )
    product = (filtered[1] * filtered[2]).astype(jnp.bfloat16)
    groups = lax.axis_size("seq")
    per_group = chan_local // groups
    pencils = lax.all_to_all(product, "seq", split_axis=0, concat_axis=1, tiled=True)
    first_chan = lax.axis_index("seq") * per_group
    life_slice = lax.dynamic_slice_in_dim(lifetimes, first_chan, per_group, 1)
    resid_slice = lax.dynamic_slice_in_dim(residues, first_chan, per_group, 1)
    convolved = modal_conv(pencils, life_slice, resid_slice).astype(jnp.bfloat16)
    returned = lax.all_to_all(convolved, "seq", split_axis=1, concat_axis=0, tiled=True)
    gated_rows = (filtered[0] * returned.astype(jnp.float32)).astype(jnp.bfloat16)
    partial = lax.dot_general(
        out_weight, gated_rows, (((0,), (0,)), ((), ())), preferred_element_type=jnp.float32
    ).astype(jnp.bfloat16)
    return reduce_scatter_chan(partial)


def solution(mesh):
    placed = (
        P(None, "chan", "seq"),
        P(None, None, "chan"),
        P(None, "chan"),
        P(None, "chan"),
        P("chan", None),
    )
    return jax.shard_map(
        local, mesh=mesh, in_specs=placed, out_specs=P("chan", "seq"), check_vma=False
    )
```

```python
import jax
import jax.numpy as jnp
from jax import lax
from jax.sharding import PartitionSpec as P


def from_behind(x, axis, by):
    devices = lax.axis_size(axis)
    pairs = [(i, i + by) for i in range(devices) if 0 <= i + by < devices]
    return lax.ppermute(x, axis, pairs)


def modal_conv(pencils, life_slice, resid_slice, block=128):
    chan_here, length = pencils.shape
    blocks = length // block
    steps = jnp.arange(block, dtype=jnp.int32).astype(jnp.float32)
    life = life_slice[:, :, None]
    resid = resid_slice[:, :, None]
    taps = jnp.sum(resid * jnp.exp(-steps[None, None, :] / life), axis=0)
    padded = jnp.concatenate([taps, jnp.zeros_like(taps)], axis=1)
    repeated = jnp.tile(padded, (1, block))[:, : block * (2 * block - 1)]
    toeplitz = repeated.reshape(chan_here, block, 2 * block - 1)[:, :, :block]
    signal = pencils.astype(jnp.float32).reshape(chan_here, blocks, block)
    precise = lax.Precision.HIGH
    inside = jnp.einsum("cnj,cjt->cnt", signal, toeplitz, precision=precise)
    to_end = jnp.exp(-(float(block - 1) - steps)[None, None, :] / life)
    leaving = jnp.einsum("cnj,rcj->rcn", signal, to_end, precision=precise)
    n_idx = jnp.arange(blocks, dtype=jnp.int32)
    gap = (n_idx[:, None] - 1 - n_idx[None, :]).astype(jnp.float32)
    exponent = jnp.where(
        (n_idx[:, None] > n_idx[None, :])[None, None],
        -float(block) * gap[None, None] / life[..., None],
        -jnp.inf,
    )
    entering = jnp.sum(jnp.exp(exponent) * leaving[:, :, None, :], axis=-1)
    from_start = resid * jnp.exp(-(steps + 1.0)[None, None, :] / life)
    carried = jnp.einsum("rcn,rct->cnt", entering, from_start, precision=precise)
    return (inside + carried).reshape(chan_here, length)


def reduce_scatter_chan(partial):
    index = lax.axis_index("chan")
    chip, core = index // 2, index % 2
    quarters = partial.reshape(2, 2, partial.shape[0] // 4, partial.shape[1])
    send = lax.dynamic_index_in_dim(quarters, 1 - core, 1, keepdims=False)
    keep = lax.dynamic_index_in_dim(quarters, core, 1, keepdims=False)
    got = lax.ppermute(send, "chan", [(j, j ^ 1) for j in range(4)])
    halves = keep.astype(jnp.float32) + got.astype(jnp.float32)
    send2 = lax.dynamic_index_in_dim(halves, 1 - chip, 0, keepdims=False).astype(jnp.bfloat16)
    keep2 = lax.dynamic_index_in_dim(halves, chip, 0, keepdims=False)
    got2 = lax.ppermute(send2, "chan", [(j, j ^ 2) for j in range(4)])
    return (keep2 + got2.astype(jnp.float32)).astype(jnp.bfloat16)


def local(qkv, taps, lifetimes, residues, out_weight):
    chan_local = qkv.shape[1]
    tok_count = qkv.shape[2]
    edge_block = qkv[:, :, tok_count - 2 :]
    earlier = from_behind(edge_block, "seq", 1)
    extended = jnp.concatenate([earlier, qkv], axis=2).astype(jnp.float32)
    filtered = (
        taps[:, 0, :, None] * extended[:, :, 2:]
        + taps[:, 1, :, None] * extended[:, :, 1:-1]
        + taps[:, 2, :, None] * extended[:, :, :-2]
    )
    product = (filtered[1] * filtered[2]).astype(jnp.bfloat16)
    groups = lax.axis_size("seq")
    per_group = chan_local // groups
    pencils = lax.all_to_all(product, "seq", split_axis=0, concat_axis=1, tiled=True)
    first_chan = lax.axis_index("seq") * per_group
    life_slice = lax.dynamic_slice_in_dim(lifetimes, first_chan, per_group, 1)
    resid_slice = lax.dynamic_slice_in_dim(residues, first_chan, per_group, 1)
    convolved = modal_conv(pencils, life_slice, resid_slice).astype(jnp.bfloat16)
    returned = lax.all_to_all(convolved, "seq", split_axis=1, concat_axis=0, tiled=True)
    gated_rows = (filtered[0] * returned.astype(jnp.float32)).astype(jnp.bfloat16)
    partial = lax.dot_general(
        out_weight, gated_rows, (((0,), (0,)), ((), ())), preferred_element_type=jnp.float32
    ).astype(jnp.bfloat16)
    return reduce_scatter_chan(partial)


def solution(mesh):
    placed = (
        P(None, "chan", "seq"),
        P(None, None, "chan"),
        P(None, "chan"),
        P(None, "chan"),
        P("chan", None),
    )
    return jax.shard_map(
        local, mesh=mesh, in_specs=placed, out_specs=P("chan", "seq"), check_vma=False
    )
```

```python
import jax
import jax.numpy as jnp
from jax import lax
from jax.sharding import PartitionSpec as P


def from_behind(x, axis, by):
    devices = lax.axis_size(axis)
    pairs = [(i, i + by) for i in range(devices) if 0 <= i + by < devices]
    return lax.ppermute(x, axis, pairs)


def modal_conv(pencils, life_slice, resid_slice, block=128):
    chan_here, length = pencils.shape
    blocks = length // block
    steps = jnp.arange(block, dtype=jnp.int32).astype(jnp.float32)
    life = life_slice[:, :, None]
    resid = resid_slice[:, :, None]
    offs = steps - float(block // 2)
    rising = resid * jnp.exp(offs[None, None, :] / life)
    falling = jnp.exp(-offs[None, None, :] / life)
    full = jnp.einsum("rcj,rct->cjt", rising, falling, precision=lax.Precision.HIGHEST)
    lag = jnp.arange(block, dtype=jnp.int32)[None, :] - jnp.arange(block, dtype=jnp.int32)[:, None]
    toeplitz = jnp.where(lag[None] >= 0, full, 0.0)
    signal = pencils.astype(jnp.float32).reshape(chan_here, blocks, block)
    precise = lax.Precision.HIGH
    inside = jnp.einsum("cnj,cjt->cnt", signal, toeplitz, precision=precise)
    to_end = jnp.exp(-(float(block - 1) - steps)[None, None, :] / life)
    leaving = jnp.einsum("cnj,rcj->rcn", signal, to_end, precision=precise)
    n_idx = jnp.arange(blocks, dtype=jnp.int32)
    gap = (n_idx[:, None] - 1 - n_idx[None, :]).astype(jnp.float32)
    exponent = jnp.where(
        (n_idx[:, None] > n_idx[None, :])[None, None],
        -float(block) * gap[None, None] / life[..., None],
        -jnp.inf,
    )
    entering = jnp.sum(jnp.exp(exponent) * leaving[:, :, None, :], axis=-1)
    from_start = resid * jnp.exp(-(steps + 1.0)[None, None, :] / life)
    carried = jnp.einsum("rcn,rct->cnt", entering, from_start, precision=precise)
    return (inside + carried).reshape(chan_here, length)


def reduce_scatter_chan(partial):
    index = lax.axis_index("chan")
    chip, core = index // 2, index % 2
    quarters = partial.reshape(partial.shape[0], 2, 2, partial.shape[1] // 4)
    send = lax.dynamic_index_in_dim(quarters, 1 - core, 2, keepdims=False)
    keep = lax.dynamic_index_in_dim(quarters, core, 2, keepdims=False)
    got = lax.ppermute(send, "chan", [(j, j ^ 1) for j in range(4)])
    halves = keep.astype(jnp.float32) + got.astype(jnp.float32)
    send2 = lax.dynamic_index_in_dim(halves, 1 - chip, 1, keepdims=False).astype(jnp.bfloat16)
    keep2 = lax.dynamic_index_in_dim(halves, chip, 1, keepdims=False)
    got2 = lax.ppermute(send2, "chan", [(j, j ^ 2) for j in range(4)])
    return (keep2 + got2.astype(jnp.float32)).astype(jnp.bfloat16).T


def local(qkv, taps, lifetimes, residues, out_weight):
    chan_local = qkv.shape[1]
    tok_count = qkv.shape[2]
    edge_block = qkv[:, :, tok_count - 2 :]
    earlier = from_behind(edge_block, "seq", 1)
    extended = jnp.concatenate([earlier, qkv], axis=2).astype(jnp.float32)
    filtered = (
        taps[:, 0, :, None] * extended[:, :, 2:]
        + taps[:, 1, :, None] * extended[:, :, 1:-1]
        + taps[:, 2, :, None] * extended[:, :, :-2]
    )
    product = (filtered[1] * filtered[2]).astype(jnp.bfloat16)
    groups = lax.axis_size("seq")
    per_group = chan_local // groups
    pencils = lax.all_to_all(product, "seq", split_axis=0, concat_axis=1, tiled=True)
    first_chan = lax.axis_index("seq") * per_group
    life_slice = lax.dynamic_slice_in_dim(lifetimes, first_chan, per_group, 1)
    resid_slice = lax.dynamic_slice_in_dim(residues, first_chan, per_group, 1)
    convolved = modal_conv(pencils, life_slice, resid_slice).astype(jnp.bfloat16)
    returned = lax.all_to_all(convolved, "seq", split_axis=1, concat_axis=0, tiled=True)
    gated_rows = (filtered[0] * returned.astype(jnp.float32)).astype(jnp.bfloat16)
    partial = lax.dot_general(
        gated_rows, out_weight, (((0,), (0,)), ((), ())), preferred_element_type=jnp.float32
    ).astype(jnp.bfloat16)
    return reduce_scatter_chan(partial)


def solution(mesh):
    placed = (
        P(None, "chan", "seq"),
        P(None, None, "chan"),
        P(None, "chan"),
        P(None, "chan"),
        P("chan", None),
    )
    return jax.shard_map(
        local, mesh=mesh, in_specs=placed, out_specs=P("chan", "seq"), check_vma=False
    )
```

```python
import jax
import jax.numpy as jnp
from jax import lax
from jax.sharding import PartitionSpec as P


def from_behind(x, axis, by):
    devices = lax.axis_size(axis)
    pairs = [(i, i + by) for i in range(devices) if 0 <= i + by < devices]
    return lax.ppermute(x, axis, pairs)


def modal_conv(pencils, life_slice, resid_slice, block=128):
    chan_here, length = pencils.shape
    blocks = length // block
    steps = jnp.arange(block, dtype=jnp.int32).astype(jnp.float32)
    life = life_slice[:, :, None]
    resid = resid_slice[:, :, None]
    offs = steps - float(block // 2)
    rising = resid * jnp.exp(offs[None, None, :] / life)
    falling = jnp.exp(-offs[None, None, :] / life)
    full = jnp.einsum("rcj,rct->cjt", rising, falling, precision=lax.Precision.HIGHEST)
    lag = jnp.arange(block, dtype=jnp.int32)[None, :] - jnp.arange(block, dtype=jnp.int32)[:, None]
    toeplitz = jnp.where(lag[None] >= 0, full, 0.0)
    signal = pencils.astype(jnp.float32).reshape(chan_here, blocks, block)
    precise = lax.Precision.HIGH
    inside = jnp.einsum("cnj,cjt->cnt", signal, toeplitz, precision=precise)
    to_end = jnp.exp(-(float(block - 1) - steps)[None, None, :] / life)
    leaving = jnp.einsum("cnj,rcj->rcn", signal, to_end, precision=precise)
    n_idx = jnp.arange(blocks, dtype=jnp.int32)
    gap = (n_idx[:, None] - 1 - n_idx[None, :]).astype(jnp.float32)
    exponent = jnp.where(
        (n_idx[:, None] > n_idx[None, :])[None, None],
        -float(block) * gap[None, None] / life[..., None],
        -jnp.inf,
    )
    entering = jnp.sum(jnp.exp(exponent) * leaving[:, :, None, :], axis=-1)
    from_start = resid * jnp.exp(-(steps + 1.0)[None, None, :] / life)
    carried = jnp.einsum("rcn,rct->cnt", entering, from_start, precision=precise)
    return (inside + carried).reshape(chan_here, length)


def reduce_scatter_chan(partial):
    index = lax.axis_index("chan")
    chip, core = index // 2, index % 2
    width = partial.shape[1] // 4
    quarter = [partial[:, q * width : (q + 1) * width] for q in range(4)]
    mine = core == 0
    send = jnp.stack([jnp.where(mine, quarter[2 * h + 1], quarter[2 * h]) for h in range(2)])
    keep = jnp.stack([jnp.where(mine, quarter[2 * h], quarter[2 * h + 1]) for h in range(2)])
    got = lax.ppermute(send, "chan", [(j, j ^ 1) for j in range(4)])
    halves = keep.astype(jnp.float32) + got.astype(jnp.float32)
    first = chip == 0
    send2 = jnp.where(first, halves[1], halves[0]).astype(jnp.bfloat16)
    keep2 = jnp.where(first, halves[0], halves[1])
    got2 = lax.ppermute(send2, "chan", [(j, j ^ 2) for j in range(4)])
    return (keep2 + got2.astype(jnp.float32)).astype(jnp.bfloat16).T


def local(qkv, taps, lifetimes, residues, out_weight):
    chan_local = qkv.shape[1]
    tok_count = qkv.shape[2]
    edge_block = qkv[:, :, tok_count - 2 :]
    earlier = from_behind(edge_block, "seq", 1)
    extended = jnp.concatenate([earlier, qkv], axis=2).astype(jnp.float32)
    filtered = (
        taps[:, 0, :, None] * extended[:, :, 2:]
        + taps[:, 1, :, None] * extended[:, :, 1:-1]
        + taps[:, 2, :, None] * extended[:, :, :-2]
    )
    product = (filtered[1] * filtered[2]).astype(jnp.bfloat16)
    groups = lax.axis_size("seq")
    per_group = chan_local // groups
    pencils = lax.all_to_all(product, "seq", split_axis=0, concat_axis=1, tiled=True)
    first_chan = lax.axis_index("seq") * per_group
    life_slice = lax.dynamic_slice_in_dim(lifetimes, first_chan, per_group, 1)
    resid_slice = lax.dynamic_slice_in_dim(residues, first_chan, per_group, 1)
    convolved = modal_conv(pencils, life_slice, resid_slice).astype(jnp.bfloat16)
    returned = lax.all_to_all(convolved, "seq", split_axis=1, concat_axis=0, tiled=True)
    gated_rows = (filtered[0] * returned.astype(jnp.float32)).astype(jnp.bfloat16)
    partial = lax.dot_general(
        gated_rows, out_weight, (((0,), (0,)), ((), ())), preferred_element_type=jnp.float32
    ).astype(jnp.bfloat16)
    return reduce_scatter_chan(partial)


def solution(mesh):
    placed = (
        P(None, "chan", "seq"),
        P(None, None, "chan"),
        P(None, "chan"),
        P(None, "chan"),
        P("chan", None),
    )
    return jax.shard_map(
        local, mesh=mesh, in_specs=placed, out_specs=P("chan", "seq"), check_vma=False
    )
```

```python
import jax
import jax.numpy as jnp
from jax import lax
from jax.sharding import PartitionSpec as P


def from_behind(x, axis, by):
    devices = lax.axis_size(axis)
    pairs = [(i, i + by) for i in range(devices) if 0 <= i + by < devices]
    return lax.ppermute(x, axis, pairs)


def modal_conv(pencils, life_slice, resid_slice):
    block = pencils.shape[2]
    steps = jnp.arange(block, dtype=jnp.int32).astype(jnp.float32)
    life = life_slice[:, :, None]
    resid = resid_slice[:, :, None]
    offs = steps - float(block // 2)
    rising = resid * jnp.exp(offs[None, None, :] / life)
    falling = jnp.exp(-offs[None, None, :] / life)
    full = jnp.einsum("rcj,rct->cjt", rising, falling, precision=lax.Precision.HIGHEST)
    lag = jnp.arange(block, dtype=jnp.int32)[None, :] - jnp.arange(block, dtype=jnp.int32)[:, None]
    toeplitz = jnp.where(lag[None] >= 0, full, 0.0)
    signal = pencils.astype(jnp.float32)
    precise = lax.Precision.HIGH
    inside = jnp.einsum("ncj,cjt->nct", signal, toeplitz, precision=precise)
    to_end = jnp.exp(-(float(block - 1) - steps)[None, None, :] / life)
    leaving = jnp.einsum("ncj,rcj->rcn", signal, to_end, precision=precise)
    blocks = signal.shape[0]
    n_idx = jnp.arange(blocks, dtype=jnp.int32)
    gap = (n_idx[None, :] - 1 - n_idx[:, None]).astype(jnp.float32)
    exponent = jnp.where(
        (n_idx[None, :] > n_idx[:, None])[None, None],
        -float(block) * gap[None, None] / life[..., None],
        -jnp.inf,
    )
    entering = jnp.sum(jnp.exp(exponent) * leaving[:, :, :, None], axis=2)
    from_start = resid * jnp.exp(-(steps + 1.0)[None, None, :] / life)
    carried = jnp.einsum("rcn,rct->nct", entering, from_start, precision=precise)
    return inside + carried


def reduce_scatter_chan(partial):
    index = lax.axis_index("chan")
    chip, core = index // 2, index % 2
    width = partial.shape[1] // 4
    quarter = [partial[:, q * width : (q + 1) * width] for q in range(4)]
    mine = core == 0
    send = jnp.stack([jnp.where(mine, quarter[2 * h + 1], quarter[2 * h]) for h in range(2)])
    keep = jnp.stack([jnp.where(mine, quarter[2 * h], quarter[2 * h + 1]) for h in range(2)])
    got = lax.ppermute(send, "chan", [(j, j ^ 1) for j in range(4)])
    halves = keep.astype(jnp.float32) + got.astype(jnp.float32)
    first = chip == 0
    send2 = jnp.where(first, halves[1], halves[0]).astype(jnp.bfloat16)
    keep2 = jnp.where(first, halves[0], halves[1])
    got2 = lax.ppermute(send2, "chan", [(j, j ^ 2) for j in range(4)])
    return (keep2 + got2.astype(jnp.float32)).astype(jnp.bfloat16).T


def local(qkv, taps, lifetimes, residues, out_weight):
    chan_local = qkv.shape[1]
    tok_count = qkv.shape[2]
    edge_block = qkv[:, :, tok_count - 2 :]
    earlier = from_behind(edge_block, "seq", 1)
    extended = jnp.concatenate([earlier, qkv], axis=2).astype(jnp.float32)
    filtered = (
        taps[:, 0, :, None] * extended[:, :, 2:]
        + taps[:, 1, :, None] * extended[:, :, 1:-1]
        + taps[:, 2, :, None] * extended[:, :, :-2]
    )
    product = (filtered[1] * filtered[2]).astype(jnp.bfloat16)
    groups = lax.axis_size("seq")
    per_group = chan_local // groups
    pencils = lax.all_to_all(
        product.reshape(groups, per_group, tok_count), "seq", split_axis=0, concat_axis=0, tiled=True
    )
    first_chan = lax.axis_index("seq") * per_group
    life_slice = lax.dynamic_slice_in_dim(lifetimes, first_chan, per_group, 1)
    resid_slice = lax.dynamic_slice_in_dim(residues, first_chan, per_group, 1)
    convolved = modal_conv(pencils, life_slice, resid_slice).astype(jnp.bfloat16)
    returned = lax.all_to_all(convolved, "seq", split_axis=0, concat_axis=0, tiled=True).reshape(
        chan_local, tok_count
    )
    gated_rows = (filtered[0] * returned.astype(jnp.float32)).astype(jnp.bfloat16)
    partial = lax.dot_general(
        gated_rows, out_weight, (((0,), (0,)), ((), ())), preferred_element_type=jnp.float32
    ).astype(jnp.bfloat16)
    return reduce_scatter_chan(partial)


def solution(mesh):
    placed = (
        P(None, "chan", "seq"),
        P(None, None, "chan"),
        P(None, "chan"),
        P(None, "chan"),
        P("chan", None),
    )
    return jax.shard_map(
        local, mesh=mesh, in_specs=placed, out_specs=P("chan", "seq"), check_vma=False
    )
```

```python
import jax
import jax.numpy as jnp
from jax import lax
from jax.sharding import PartitionSpec as P


def from_behind(x, axis, by):
    devices = lax.axis_size(axis)
    pairs = [(i, i + by) for i in range(devices) if 0 <= i + by < devices]
    return lax.ppermute(x, axis, pairs)


def modal_conv(pencils, life_slice, resid_slice):
    block = pencils.shape[2]
    steps = jnp.arange(block, dtype=jnp.int32).astype(jnp.float32)
    life = life_slice[:, :, None]
    resid = resid_slice[:, :, None]
    offs = steps - float(block // 2)
    rising = resid * jnp.exp(offs[None, None, :] / life)
    falling = jnp.exp(-offs[None, None, :] / life)
    full = jnp.einsum("rcj,rct->cjt", rising, falling, precision=lax.Precision.HIGHEST)
    lag = jnp.arange(block, dtype=jnp.int32)[None, :] - jnp.arange(block, dtype=jnp.int32)[:, None]
    toeplitz = jnp.where(lag[None] >= 0, full, 0.0)
    signal = pencils.astype(jnp.float32)
    precise = lax.Precision.HIGH
    inside = jnp.einsum("ncj,cjt->nct", signal, toeplitz, precision=precise)
    to_end = jnp.exp(-(float(block - 1) - steps)[None, None, :] / life)
    leaving = jnp.einsum("ncj,rcj->rcn", signal, to_end, precision=precise)
    blocks = signal.shape[0]
    n_idx = jnp.arange(blocks, dtype=jnp.int32)
    gap = (n_idx[None, :] - 1 - n_idx[:, None]).astype(jnp.float32)
    exponent = jnp.where(
        (n_idx[None, :] > n_idx[:, None])[None, None],
        -float(block) * gap[None, None] / life[..., None],
        -jnp.inf,
    )
    entering = jnp.sum(jnp.exp(exponent) * leaving[:, :, :, None], axis=2)
    from_start = resid * jnp.exp(-(steps + 1.0)[None, None, :] / life)
    carried = jnp.einsum("rcn,rct->nct", entering, from_start, precision=precise)
    return inside + carried


def reduce_scatter_chan(partial):
    index = lax.axis_index("chan")
    chip, core = index // 2, index % 2
    width = partial.shape[1] // 4
    quarter = [partial[:, q * width : (q + 1) * width] for q in range(4)]
    mine = core == 0
    send = jnp.stack([jnp.where(mine, quarter[2 * h + 1], quarter[2 * h]) for h in range(2)])
    keep = jnp.stack([jnp.where(mine, quarter[2 * h], quarter[2 * h + 1]) for h in range(2)])
    got = lax.ppermute(send, "chan", [(j, j ^ 1) for j in range(4)])
    halves = keep.astype(jnp.float32) + got.astype(jnp.float32)
    first = chip == 0
    send2 = jnp.where(first, halves[1], halves[0]).astype(jnp.bfloat16)
    keep2 = jnp.where(first, halves[0], halves[1])
    got2 = lax.ppermute(send2, "chan", [(j, j ^ 2) for j in range(4)])
    return (keep2 + got2.astype(jnp.float32)).astype(jnp.bfloat16).T


def local(qkv, taps, lifetimes, residues, out_weight):
    chan_local = qkv.shape[1]
    tok_count = qkv.shape[2]
    edge_block = qkv[:, :, tok_count - 2 :]
    earlier = from_behind(edge_block, "seq", 1)

    def short_filter(stream):
        signal = qkv[stream].astype(jnp.float32)
        back1 = jnp.concatenate([earlier[stream, :, 1:], qkv[stream, :, :-1]], axis=1)
        back2 = jnp.concatenate([earlier[stream], qkv[stream, :, :-2]], axis=1)
        return (
            taps[stream, 0][:, None] * signal
            + taps[stream, 1][:, None] * back1.astype(jnp.float32)
            + taps[stream, 2][:, None] * back2.astype(jnp.float32)
        )

    product = (short_filter(1) * short_filter(2)).astype(jnp.bfloat16)
    groups = lax.axis_size("seq")
    per_group = chan_local // groups
    pencils = lax.all_to_all(
        product.reshape(groups, per_group, tok_count), "seq", split_axis=0, concat_axis=0, tiled=True
    )
    first_chan = lax.axis_index("seq") * per_group
    life_slice = lax.dynamic_slice_in_dim(lifetimes, first_chan, per_group, 1)
    resid_slice = lax.dynamic_slice_in_dim(residues, first_chan, per_group, 1)
    convolved = modal_conv(pencils, life_slice, resid_slice).astype(jnp.bfloat16)
    returned = lax.all_to_all(convolved, "seq", split_axis=0, concat_axis=0, tiled=True).reshape(
        chan_local, tok_count
    )
    gated_rows = (short_filter(0) * returned.astype(jnp.float32)).astype(jnp.bfloat16)
    partial = lax.dot_general(
        gated_rows, out_weight, (((0,), (0,)), ((), ())), preferred_element_type=jnp.float32
    ).astype(jnp.bfloat16)
    return reduce_scatter_chan(partial)


def solution(mesh):
    placed = (
        P(None, "chan", "seq"),
        P(None, None, "chan"),
        P(None, "chan"),
        P(None, "chan"),
        P("chan", None),
    )
    return jax.shard_map(
        local, mesh=mesh, in_specs=placed, out_specs=P("chan", "seq"), check_vma=False
    )
```

```python
import jax
import jax.numpy as jnp
from jax import lax
from jax.sharding import PartitionSpec as P


def from_behind(x, axis, by):
    devices = lax.axis_size(axis)
    pairs = [(i, i + by) for i in range(devices) if 0 <= i + by < devices]
    return lax.ppermute(x, axis, pairs)


def exclusive_decay(states, life, stride):
    count = states.shape[-1]
    idx = jnp.arange(count, dtype=jnp.int32)
    gap = (idx[:, None] - 1 - idx[None, :]).astype(jnp.float32)
    extra = states.ndim - 3
    scale = life.reshape(life.shape[:2] + (1,) * (extra + 2))
    exponent = jnp.where(idx[:, None] > idx[None, :], -stride * gap / scale, -jnp.inf)
    return jnp.sum(jnp.exp(exponent) * states[..., None, :], axis=-1)


def state_scan(leaving, life, block):
    modes, chan, blocks = leaving.shape
    inner = 8 if blocks % 8 == 0 else 1
    outer = blocks // inner
    grouped = leaving.reshape(modes, chan, outer, inner)
    within = exclusive_decay(grouped, life, block)
    to_group_end = jnp.exp(
        -block * (float(inner - 1) - jnp.arange(inner, dtype=jnp.int32).astype(jnp.float32))
        / life
    )
    totals = jnp.sum(to_group_end[:, :, None, :] * grouped, axis=-1)
    before = exclusive_decay(totals, life, block * inner)
    into = jnp.exp(-block * jnp.arange(inner, dtype=jnp.int32).astype(jnp.float32) / life)
    result = within + into[:, :, None, :] * before[..., None]
    return result.reshape(modes, chan, blocks)


def modal_conv(pencils, life_slice, resid_slice, block=128):
    chan_here, length = pencils.shape
    blocks = length // block
    steps = jnp.arange(block, dtype=jnp.int32).astype(jnp.float32)
    life = life_slice[:, :, None]
    resid = resid_slice[:, :, None]
    offs = steps - float(block // 2)
    rising = resid * jnp.exp(offs[None, None, :] / life)
    falling = jnp.exp(-offs[None, None, :] / life)
    full = jnp.einsum("rcj,rct->cjt", rising, falling, precision=lax.Precision.HIGHEST)
    lag = jnp.arange(block, dtype=jnp.int32)[None, :] - jnp.arange(block, dtype=jnp.int32)[:, None]
    toeplitz = jnp.where(lag[None] >= 0, full, 0.0)
    signal = pencils.astype(jnp.float32).reshape(chan_here, blocks, block)
    precise = lax.Precision.HIGH
    inside = jnp.einsum("cnj,cjt->cnt", signal, toeplitz, precision=precise)
    to_end = jnp.exp(-(float(block - 1) - steps)[None, None, :] / life)
    leaving = jnp.einsum("cnj,rcj->rcn", signal, to_end, precision=precise)
    entering = state_scan(leaving, life, float(block))
    from_start = resid * jnp.exp(-(steps + 1.0)[None, None, :] / life)
    carried = jnp.einsum("rcn,rct->cnt", entering, from_start, precision=precise)
    return (inside + carried).reshape(chan_here, length)


def reduce_scatter_chan(partial):
    index = lax.axis_index("chan")
    chip, core = index // 2, index % 2
    width = partial.shape[1] // 4
    quarter = [partial[:, q * width : (q + 1) * width] for q in range(4)]
    mine = core == 0
    send = jnp.stack([jnp.where(mine, quarter[2 * h + 1], quarter[2 * h]) for h in range(2)])
    keep = jnp.stack([jnp.where(mine, quarter[2 * h], quarter[2 * h + 1]) for h in range(2)])
    got = lax.ppermute(send, "chan", [(j, j ^ 1) for j in range(4)])
    halves = keep.astype(jnp.float32) + got.astype(jnp.float32)
    first = chip == 0
    send2 = jnp.where(first, halves[1], halves[0]).astype(jnp.bfloat16)
    keep2 = jnp.where(first, halves[0], halves[1])
    got2 = lax.ppermute(send2, "chan", [(j, j ^ 2) for j in range(4)])
    return (keep2 + got2.astype(jnp.float32)).astype(jnp.bfloat16).T


def local(qkv, taps, lifetimes, residues, out_weight):
    chan_local = qkv.shape[1]
    tok_count = qkv.shape[2]
    edge_block = qkv[:, :, tok_count - 2 :]
    earlier = from_behind(edge_block, "seq", 1)
    extended = jnp.concatenate([earlier, qkv], axis=2).astype(jnp.float32)
    filtered = (
        taps[:, 0, :, None] * extended[:, :, 2:]
        + taps[:, 1, :, None] * extended[:, :, 1:-1]
        + taps[:, 2, :, None] * extended[:, :, :-2]
    )
    product = (filtered[1] * filtered[2]).astype(jnp.bfloat16)
    groups = lax.axis_size("seq")
    per_group = chan_local // groups
    pencils = lax.all_to_all(product, "seq", split_axis=0, concat_axis=1, tiled=True)
    first_chan = lax.axis_index("seq") * per_group
    life_slice = lax.dynamic_slice_in_dim(lifetimes, first_chan, per_group, 1)
    resid_slice = lax.dynamic_slice_in_dim(residues, first_chan, per_group, 1)
    convolved = modal_conv(pencils, life_slice, resid_slice).astype(jnp.bfloat16)
    returned = lax.all_to_all(convolved, "seq", split_axis=1, concat_axis=0, tiled=True)
    gated_rows = (filtered[0] * returned.astype(jnp.float32)).astype(jnp.bfloat16)
    partial = lax.dot_general(
        gated_rows, out_weight, (((0,), (0,)), ((), ())), preferred_element_type=jnp.float32
    ).astype(jnp.bfloat16)
    return reduce_scatter_chan(partial)


def solution(mesh):
    placed = (
        P(None, "chan", "seq"),
        P(None, None, "chan"),
        P(None, "chan"),
        P(None, "chan"),
        P("chan", None),
    )
    return jax.shard_map(
        local, mesh=mesh, in_specs=placed, out_specs=P("chan", "seq"), check_vma=False
    )
```

```python
import jax
import jax.numpy as jnp
from jax import lax
from jax.sharding import PartitionSpec as P


def from_behind(x, axis, by):
    devices = lax.axis_size(axis)
    pairs = [(i, i + by) for i in range(devices) if 0 <= i + by < devices]
    return lax.ppermute(x, axis, pairs)


def modal_conv(pencils, life_slice, resid_slice, block=128):
    chan_here, length = pencils.shape
    blocks = length // block
    steps = jnp.arange(block, dtype=jnp.int32).astype(jnp.float32)
    life = life_slice[:, :, None]
    resid = resid_slice[:, :, None]
    offs = steps - float(block // 2)
    rising = resid * jnp.exp(offs[None, None, :] / life)
    falling = jnp.exp(-offs[None, None, :] / life)
    full = jnp.einsum("rcj,rct->cjt", rising, falling, precision=lax.Precision.HIGHEST)
    lag = jnp.arange(block, dtype=jnp.int32)[None, :] - jnp.arange(block, dtype=jnp.int32)[:, None]
    toeplitz = jnp.where(lag[None] >= 0, full, 0.0)
    signal = pencils.astype(jnp.float32).reshape(chan_here, blocks, block)
    precise = lax.Precision.HIGH
    inside = jnp.einsum("cnj,cjt->cnt", signal, toeplitz, precision=precise)
    to_end = jnp.exp(-(float(block - 1) - steps)[None, None, :] / life)
    leaving = jnp.einsum("cnj,rcj->rcn", signal, to_end, precision=precise)
    n_idx = jnp.arange(blocks, dtype=jnp.int32)
    gap = (n_idx[:, None] - 1 - n_idx[None, :]).astype(jnp.float32)
    exponent = jnp.where(
        (n_idx[:, None] > n_idx[None, :])[None, None],
        -float(block) * gap[None, None] / life[..., None],
        -jnp.inf,
    )
    entering = jnp.sum(jnp.exp(exponent) * leaving[:, :, None, :], axis=-1)
    from_start = resid * jnp.exp(-(steps + 1.0)[None, None, :] / life)
    carried = jnp.einsum("rcn,rct->cnt", entering, from_start, precision=precise)
    return (inside + carried).reshape(chan_here, length)


def reduce_scatter_chan(partial):
    index = lax.axis_index("chan")
    chip, core = index // 2, index % 2
    width = partial.shape[1] // 4
    quarter = [partial[:, q * width : (q + 1) * width] for q in range(4)]
    mine = core == 0
    send = jnp.stack([jnp.where(mine, quarter[2 * h + 1], quarter[2 * h]) for h in range(2)])
    keep = jnp.stack([jnp.where(mine, quarter[2 * h], quarter[2 * h + 1]) for h in range(2)])
    got = lax.ppermute(send, "chan", [(j, j ^ 1) for j in range(4)])
    halves = keep.astype(jnp.float32) + got.astype(jnp.float32)
    first = chip == 0
    send2 = jnp.where(first, halves[1], halves[0]).astype(jnp.bfloat16)
    keep2 = jnp.where(first, halves[0], halves[1])
    got2 = lax.ppermute(send2, "chan", [(j, j ^ 2) for j in range(4)])
    return (keep2 + got2.astype(jnp.float32)).astype(jnp.bfloat16).T


def local(qkv, taps, lifetimes, residues, out_weight):
    chan_local = qkv.shape[1]
    tok_count = qkv.shape[2]
    pick = (
        jnp.arange(tok_count, dtype=jnp.int32)[:, None]
        == tok_count - 2 + jnp.arange(2, dtype=jnp.int32)[None, :]
    ).astype(qkv.dtype)
    edge_block = jnp.einsum(
        "sct,tk->skc", qkv, pick, preferred_element_type=jnp.float32
    ).astype(qkv.dtype)
    earlier = jnp.swapaxes(from_behind(edge_block, "seq", 1), 1, 2)
    extended = jnp.concatenate([earlier, qkv], axis=2).astype(jnp.float32)
    filtered = (
        taps[:, 0, :, None] * extended[:, :, 2:]
        + taps[:, 1, :, None] * extended[:, :, 1:-1]
        + taps[:, 2, :, None] * extended[:, :, :-2]
    )
    product = (filtered[1] * filtered[2]).astype(jnp.bfloat16)
    groups = lax.axis_size("seq")
    per_group = chan_local // groups
    pencils = lax.all_to_all(product, "seq", split_axis=0, concat_axis=1, tiled=True)
    first_chan = lax.axis_index("seq") * per_group
    life_slice = lax.dynamic_slice_in_dim(lifetimes, first_chan, per_group, 1)
    resid_slice = lax.dynamic_slice_in_dim(residues, first_chan, per_group, 1)
    convolved = modal_conv(pencils, life_slice, resid_slice).astype(jnp.bfloat16)
    returned = lax.all_to_all(convolved, "seq", split_axis=1, concat_axis=0, tiled=True)
    gated_rows = (filtered[0] * returned.astype(jnp.float32)).astype(jnp.bfloat16)
    partial = lax.dot_general(
        gated_rows, out_weight, (((0,), (0,)), ((), ())), preferred_element_type=jnp.float32
    ).astype(jnp.bfloat16)
    return reduce_scatter_chan(partial)


def solution(mesh):
    placed = (
        P(None, "chan", "seq"),
        P(None, None, "chan"),
        P(None, "chan"),
        P(None, "chan"),
        P("chan", None),
    )
    return jax.shard_map(
        local, mesh=mesh, in_specs=placed, out_specs=P("chan", "seq"), check_vma=False
    )
```

```python
import jax
import jax.numpy as jnp
from jax import lax
from jax.sharding import PartitionSpec as P


def from_behind(x, axis, by):
    devices = lax.axis_size(axis)
    pairs = [(i, i + by) for i in range(devices) if 0 <= i + by < devices]
    return lax.ppermute(x, axis, pairs)


def modal_conv(pencils, life_slice, resid_slice, block=128):
    chan_here, length = pencils.shape
    blocks = length // block
    steps = jnp.arange(block, dtype=jnp.int32).astype(jnp.float32)
    life = life_slice[:, :, None]
    resid = resid_slice[:, :, None]
    offs = steps - float(block // 2)
    rising = resid * jnp.exp(offs[None, None, :] / life)
    falling = jnp.exp(-offs[None, None, :] / life)
    full = jnp.einsum("rcj,rct->cjt", rising, falling, precision=lax.Precision.HIGHEST)
    lag = jnp.arange(block, dtype=jnp.int32)[None, :] - jnp.arange(block, dtype=jnp.int32)[:, None]
    toeplitz = jnp.where(lag[None] >= 0, full, 0.0)
    signal = pencils.astype(jnp.float32).reshape(chan_here, blocks, block)
    precise = lax.Precision.HIGH
    inside = jnp.einsum("cnj,cjt->cnt", signal, toeplitz, precision=precise)
    to_end = jnp.exp(-(float(block - 1) - steps)[None, None, :] / life)
    leaving = jnp.einsum("cnj,rcj->rcn", signal, to_end, precision=precise)
    n_idx = jnp.arange(blocks, dtype=jnp.int32)
    gap = (n_idx[:, None] - 1 - n_idx[None, :]).astype(jnp.float32)
    exponent = jnp.where(
        (n_idx[:, None] > n_idx[None, :])[None, None],
        -float(block) * gap[None, None] / life[..., None],
        -jnp.inf,
    )
    entering = jnp.sum(jnp.exp(exponent) * leaving[:, :, None, :], axis=-1)
    from_start = resid * jnp.exp(-(steps + 1.0)[None, None, :] / life)
    carried = jnp.einsum("rcn,rct->cnt", entering, from_start, precision=precise)
    return (inside + carried).reshape(chan_here, length)


def reduce_scatter_chan(partial):
    index = lax.axis_index("chan")
    chip, core = index // 2, index % 2
    width = partial.shape[1] // 4
    quarter = [partial[:, q * width : (q + 1) * width] for q in range(4)]
    mine = core == 0
    send = jnp.stack([jnp.where(mine, quarter[2 * h + 1], quarter[2 * h]) for h in range(2)])
    keep = jnp.stack([jnp.where(mine, quarter[2 * h], quarter[2 * h + 1]) for h in range(2)])
    got = lax.ppermute(send, "chan", [(j, j ^ 1) for j in range(4)])
    halves = keep.astype(jnp.float32) + got.astype(jnp.float32)
    first = chip == 0
    send2 = jnp.where(first, halves[1], halves[0]).astype(jnp.bfloat16)
    keep2 = jnp.where(first, halves[0], halves[1])
    got2 = lax.ppermute(send2, "chan", [(j, j ^ 2) for j in range(4)])
    return (keep2 + got2.astype(jnp.float32)).astype(jnp.bfloat16).T


def local(qkv, taps, lifetimes, residues, out_weight):
    chan_local = qkv.shape[1]
    tok_count = qkv.shape[2]
    edge_block = qkv[:, :, tok_count - 2 :]
    earlier = from_behind(edge_block, "seq", 1)

    signal = qkv.astype(jnp.float32)
    pad1 = jnp.zeros(signal.shape[:2] + (1,), jnp.float32)
    pad2 = jnp.zeros(signal.shape[:2] + (2,), jnp.float32)
    no_halo = (
        taps[:, 0, :, None] * signal
        + taps[:, 1, :, None] * jnp.concatenate([pad1, signal[:, :, :-1]], axis=2)
        + taps[:, 2, :, None] * jnp.concatenate([pad2, signal[:, :, :-2]], axis=2)
    )
    head_in = jnp.concatenate([earlier, qkv[:, :, :2]], axis=2).astype(jnp.float32)
    head = (
        taps[:, 0, :, None] * head_in[:, :, 2:]
        + taps[:, 1, :, None] * head_in[:, :, 1:3]
        + taps[:, 2, :, None] * head_in[:, :, :2]
    )
    product = lax.dynamic_update_slice(
        (no_halo[1] * no_halo[2]).astype(jnp.bfloat16),
        (head[1] * head[2]).astype(jnp.bfloat16),
        (0, 0),
    )
    filtered_q = lax.dynamic_update_slice(no_halo[0], head[0], (0, 0))
    groups = lax.axis_size("seq")
    per_group = chan_local // groups
    pencils = lax.all_to_all(product, "seq", split_axis=0, concat_axis=1, tiled=True)
    first_chan = lax.axis_index("seq") * per_group
    life_slice = lax.dynamic_slice_in_dim(lifetimes, first_chan, per_group, 1)
    resid_slice = lax.dynamic_slice_in_dim(residues, first_chan, per_group, 1)
    convolved = modal_conv(pencils, life_slice, resid_slice).astype(jnp.bfloat16)
    returned = lax.all_to_all(convolved, "seq", split_axis=1, concat_axis=0, tiled=True)
    gated_rows = (filtered_q * returned.astype(jnp.float32)).astype(jnp.bfloat16)
    partial = lax.dot_general(
        gated_rows, out_weight, (((0,), (0,)), ((), ())), preferred_element_type=jnp.float32
    ).astype(jnp.bfloat16)
    return reduce_scatter_chan(partial)


def solution(mesh):
    placed = (
        P(None, "chan", "seq"),
        P(None, None, "chan"),
        P(None, "chan"),
        P(None, "chan"),
        P("chan", None),
    )
    return jax.shard_map(
        local, mesh=mesh, in_specs=placed, out_specs=P("chan", "seq"), check_vma=False
    )
```

```python
import jax
import jax.numpy as jnp
from jax import lax
from jax.sharding import PartitionSpec as P


def from_behind(x, axis, by):
    devices = lax.axis_size(axis)
    pairs = [(i, i + by) for i in range(devices) if 0 <= i + by < devices]
    return lax.ppermute(x, axis, pairs)


def modal_conv(pencils, life_slice, resid_slice):
    block = pencils.shape[2]
    steps = jnp.arange(block, dtype=jnp.int32).astype(jnp.float32)
    life = life_slice[:, :, None]
    resid = resid_slice[:, :, None]
    offs = steps - float(block // 2)
    rising = resid * jnp.exp(offs[None, None, :] / life)
    falling = jnp.exp(-offs[None, None, :] / life)
    full = jnp.einsum("rcj,rct->cjt", rising, falling, precision=lax.Precision.HIGHEST)
    lag = jnp.arange(block, dtype=jnp.int32)[None, :] - jnp.arange(block, dtype=jnp.int32)[:, None]
    toeplitz = jnp.where(lag[None] >= 0, full, 0.0)
    signal = pencils.astype(jnp.float32)
    precise = lax.Precision.HIGH
    inside = jnp.einsum("ncj,cjt->nct", signal, toeplitz, precision=precise)
    to_end = jnp.exp(-(float(block - 1) - steps)[None, None, :] / life)
    leaving = jnp.einsum("ncj,rcj->rcn", signal, to_end, precision=precise)
    blocks = signal.shape[0]
    n_idx = jnp.arange(blocks, dtype=jnp.int32)
    gap = (n_idx[:, None] - 1 - n_idx[None, :]).astype(jnp.float32)
    exponent = jnp.where(
        (n_idx[:, None] > n_idx[None, :])[None, None],
        -float(block) * gap[None, None] / life[..., None],
        -jnp.inf,
    )
    entering = jnp.sum(jnp.exp(exponent) * leaving[:, :, None, :], axis=-1)
    from_start = resid * jnp.exp(-(steps + 1.0)[None, None, :] / life)
    carried = jnp.einsum("rcn,rct->nct", entering, from_start, precision=precise)
    return inside + carried


def reduce_scatter_chan(partial):
    index = lax.axis_index("chan")
    chip, core = index // 2, index % 2
    width = partial.shape[1] // 4
    quarter = [partial[:, q * width : (q + 1) * width] for q in range(4)]
    mine = core == 0
    send = jnp.stack([jnp.where(mine, quarter[2 * h + 1], quarter[2 * h]) for h in range(2)])
    keep = jnp.stack([jnp.where(mine, quarter[2 * h], quarter[2 * h + 1]) for h in range(2)])
    got = lax.ppermute(send, "chan", [(j, j ^ 1) for j in range(4)])
    halves = keep.astype(jnp.float32) + got.astype(jnp.float32)
    first = chip == 0
    send2 = jnp.where(first, halves[1], halves[0]).astype(jnp.bfloat16)
    keep2 = jnp.where(first, halves[0], halves[1])
    got2 = lax.ppermute(send2, "chan", [(j, j ^ 2) for j in range(4)])
    return (keep2 + got2.astype(jnp.float32)).astype(jnp.bfloat16).T


def pack_rows(values, width):
    groups, count = values.shape
    rows = -(-count // width)
    padded = jnp.pad(values, ((0, 0), (0, rows * width - count)))
    return padded.reshape(groups, rows, width)


def local(qkv, taps, lifetimes, residues, out_weight):
    chan_local = qkv.shape[1]
    tok_count = qkv.shape[2]
    groups = lax.axis_size("seq")
    per_group = chan_local // groups

    signal = qkv[1:].astype(jnp.float32)
    pad1 = jnp.zeros(signal.shape[:2] + (1,), jnp.float32)
    pad2 = jnp.zeros(signal.shape[:2] + (2,), jnp.float32)
    no_halo = (
        taps[1:, 0, :, None] * signal
        + taps[1:, 1, :, None] * jnp.concatenate([pad1, signal[:, :, :-1]], axis=2)
        + taps[1:, 2, :, None] * jnp.concatenate([pad2, signal[:, :, :-2]], axis=2)
    )
    product = (no_halo[0] * no_halo[1]).astype(jnp.bfloat16)
    ends = jnp.concatenate([qkv[1:, :, :2], qkv[1:, :, tok_count - 2 :]], axis=2)
    edges = jnp.concatenate(
        [jnp.swapaxes(ends, 0, 1).reshape(chan_local, 8), qkv[0, :, tok_count - 2 :]], axis=1
    )
    edge_count = edges.shape[1]
    payload = jnp.concatenate(
        [
            product.reshape(groups, per_group, tok_count),
            pack_rows(edges.reshape(groups, per_group * edge_count), tok_count),
        ],
        axis=1,
    )
    arrived = lax.all_to_all(payload, "seq", split_axis=0, concat_axis=0, tiled=True)
    first_chan = lax.axis_index("seq") * per_group
    life_slice = lax.dynamic_slice_in_dim(lifetimes, first_chan, per_group, 1)
    resid_slice = lax.dynamic_slice_in_dim(residues, first_chan, per_group, 1)
    tap_slice = lax.dynamic_slice_in_dim(taps, first_chan, per_group, 2)

    got_edges = (
        arrived[:, per_group:, :]
        .reshape(groups, -1)[:, : per_group * edge_count]
        .reshape(groups, per_group, edge_count)
        .astype(jnp.float32)
    )
    before = jnp.concatenate([jnp.zeros_like(got_edges[:1]), got_edges[:-1]], axis=0)

    def head(stream, at):
        t0, t1, t2 = (tap_slice[stream, i][None, :] for i in range(3))
        x0, x1 = got_edges[..., at], got_edges[..., at + 1]
        m2, m1 = before[..., at + 2], before[..., at + 3]
        return jnp.stack([t0 * x0 + t1 * m1 + t2 * m2, t0 * x1 + t1 * x0 + t2 * m1], axis=-1)

    fixed = (head(1, 0) * head(2, 4)).astype(jnp.bfloat16)
    pencils = jnp.concatenate([fixed, arrived[:, :per_group, 2:]], axis=2)
    convolved = modal_conv(pencils, life_slice, resid_slice).astype(jnp.bfloat16)
    q_before = before[..., 8:10].astype(jnp.bfloat16).reshape(groups, per_group * 2)
    back = jnp.concatenate([convolved, pack_rows(q_before, tok_count)], axis=1)
    returned = lax.all_to_all(back, "seq", split_axis=0, concat_axis=0, tiled=True)
    conv_rows = returned[:, :per_group, :].reshape(chan_local, tok_count)
    q_halo = returned[:, per_group, : per_group * 2].reshape(chan_local, 2)
    extended = jnp.concatenate([q_halo, qkv[0]], axis=1).astype(jnp.float32)
    filtered_q = (
        taps[0, 0, :, None] * extended[:, 2:]
        + taps[0, 1, :, None] * extended[:, 1:-1]
        + taps[0, 2, :, None] * extended[:, :-2]
    )
    gated_rows = (filtered_q * conv_rows.astype(jnp.float32)).astype(jnp.bfloat16)
    partial = lax.dot_general(
        gated_rows, out_weight, (((0,), (0,)), ((), ())), preferred_element_type=jnp.float32
    ).astype(jnp.bfloat16)
    return reduce_scatter_chan(partial)


def solution(mesh):
    placed = (
        P(None, "chan", "seq"),
        P(None, None, "chan"),
        P(None, "chan"),
        P(None, "chan"),
        P("chan", None),
    )
    return jax.shard_map(
        local, mesh=mesh, in_specs=placed, out_specs=P("chan", "seq"), check_vma=False
    )
```

```python
import jax
import jax.numpy as jnp
from jax import lax
from jax.experimental import pallas as pl
from jax.sharding import PartitionSpec as P


def from_behind(x, axis, by):
    devices = lax.axis_size(axis)
    pairs = [(i, i + by) for i in range(devices) if 0 <= i + by < devices]
    return lax.ppermute(x, axis, pairs)


def modal_conv(pencils, life_slice, resid_slice, block=128):
    chan_here, length = pencils.shape
    blocks = length // block
    steps = jnp.arange(block, dtype=jnp.int32).astype(jnp.float32)
    life = life_slice[:, :, None]
    resid = resid_slice[:, :, None]
    offs = steps - float(block // 2)
    rising = resid * jnp.exp(offs[None, None, :] / life)
    falling = jnp.exp(-offs[None, None, :] / life)
    full = jnp.einsum("rcj,rct->cjt", rising, falling, precision=lax.Precision.HIGHEST)
    lag = jnp.arange(block, dtype=jnp.int32)[None, :] - jnp.arange(block, dtype=jnp.int32)[:, None]
    toeplitz = jnp.where(lag[None] >= 0, full, 0.0)
    signal = pencils.astype(jnp.float32).reshape(chan_here, blocks, block)
    precise = lax.Precision.HIGH
    inside = jnp.einsum("cnj,cjt->cnt", signal, toeplitz, precision=precise)
    to_end = jnp.exp(-(float(block - 1) - steps)[None, None, :] / life)
    leaving = jnp.einsum("cnj,rcj->rcn", signal, to_end, precision=precise)
    n_idx = jnp.arange(blocks, dtype=jnp.int32)
    gap = (n_idx[:, None] - 1 - n_idx[None, :]).astype(jnp.float32)
    exponent = jnp.where(
        (n_idx[:, None] > n_idx[None, :])[None, None],
        -float(block) * gap[None, None] / life[..., None],
        -jnp.inf,
    )
    entering = jnp.sum(jnp.exp(exponent) * leaving[:, :, None, :], axis=-1)
    from_start = resid * jnp.exp(-(steps + 1.0)[None, None, :] / life)
    carried = jnp.einsum("rcn,rct->cnt", entering, from_start, precision=precise)
    return (inside + carried).reshape(chan_here, length)


def reduce_scatter_chan(partial):
    index = lax.axis_index("chan")
    chip, core = index // 2, index % 2
    width = partial.shape[1] // 4
    quarter = [partial[:, q * width : (q + 1) * width] for q in range(4)]
    mine = core == 0
    send = jnp.stack([jnp.where(mine, quarter[2 * h + 1], quarter[2 * h]) for h in range(2)])
    keep = jnp.stack([jnp.where(mine, quarter[2 * h], quarter[2 * h + 1]) for h in range(2)])
    got = lax.ppermute(send, "chan", [(j, j ^ 1) for j in range(4)])
    halves = keep.astype(jnp.float32) + got.astype(jnp.float32)
    first = chip == 0
    send2 = jnp.where(first, halves[1], halves[0]).astype(jnp.bfloat16)
    keep2 = jnp.where(first, halves[0], halves[1])
    got2 = lax.ppermute(send2, "chan", [(j, j ^ 2) for j in range(4)])
    return (keep2 + got2.astype(jnp.float32)).astype(jnp.bfloat16).T


def project_kernel(gated_ref, weight_ref, out_ref):
    out_ref[...] = lax.dot_general(
        gated_ref[...], weight_ref[...], (((0,), (0,)), ((), ())),
        preferred_element_type=jnp.float32,
    ).astype(out_ref.dtype)


def project(gated_rows, out_weight, cols=512):
    chans, toks = gated_rows.shape
    outs = out_weight.shape[1]
    return pl.pallas_call(
        project_kernel,
        grid=(outs // cols,),
        in_specs=[
            pl.BlockSpec((chans, toks), lambda j: (0, 0)),
            pl.BlockSpec((chans, cols), lambda j: (0, j)),
        ],
        out_specs=pl.BlockSpec((toks, cols), lambda j: (0, j)),
        out_shape=jax.ShapeDtypeStruct((toks, outs), jnp.bfloat16),
    )(gated_rows, out_weight)


def local(qkv, taps, lifetimes, residues, out_weight):
    chan_local = qkv.shape[1]
    tok_count = qkv.shape[2]
    edge_block = qkv[:, :, tok_count - 2 :]
    earlier = from_behind(edge_block, "seq", 1)
    extended = jnp.concatenate([earlier, qkv], axis=2).astype(jnp.float32)
    filtered = (
        taps[:, 0, :, None] * extended[:, :, 2:]
        + taps[:, 1, :, None] * extended[:, :, 1:-1]
        + taps[:, 2, :, None] * extended[:, :, :-2]
    )
    product = (filtered[1] * filtered[2]).astype(jnp.bfloat16)
    groups = lax.axis_size("seq")
    per_group = chan_local // groups
    pencils = lax.all_to_all(product, "seq", split_axis=0, concat_axis=1, tiled=True)
    first_chan = lax.axis_index("seq") * per_group
    life_slice = lax.dynamic_slice_in_dim(lifetimes, first_chan, per_group, 1)
    resid_slice = lax.dynamic_slice_in_dim(residues, first_chan, per_group, 1)
    convolved = modal_conv(pencils, life_slice, resid_slice).astype(jnp.bfloat16)
    returned = lax.all_to_all(convolved, "seq", split_axis=1, concat_axis=0, tiled=True)
    gated_rows = (filtered[0] * returned.astype(jnp.float32)).astype(jnp.bfloat16)
    partial = project(gated_rows, out_weight)
    return reduce_scatter_chan(partial)


def solution(mesh):
    placed = (
        P(None, "chan", "seq"),
        P(None, None, "chan"),
        P(None, "chan"),
        P(None, "chan"),
        P("chan", None),
    )
    return jax.shard_map(
        local, mesh=mesh, in_specs=placed, out_specs=P("chan", "seq"), check_vma=False
    )
```

```python
import jax
import jax.numpy as jnp
from jax import lax
from jax.experimental import pallas as pl
from jax.experimental.pallas import tpu as pltpu
from jax.sharding import PartitionSpec as P


def from_behind(x, axis, by):
    devices = lax.axis_size(axis)
    pairs = [(i, i + by) for i in range(devices) if 0 <= i + by < devices]
    return lax.ppermute(x, axis, pairs)


def modal_conv(pencils, life_slice, resid_slice, block=128):
    chan_here, length = pencils.shape
    blocks = length // block
    steps = jnp.arange(block, dtype=jnp.int32).astype(jnp.float32)
    life = life_slice[:, :, None]
    resid = resid_slice[:, :, None]
    offs = steps - float(block // 2)
    rising = resid * jnp.exp(offs[None, None, :] / life)
    falling = jnp.exp(-offs[None, None, :] / life)
    full = jnp.einsum("rcj,rct->cjt", rising, falling, precision=lax.Precision.HIGHEST)
    lag = jnp.arange(block, dtype=jnp.int32)[None, :] - jnp.arange(block, dtype=jnp.int32)[:, None]
    toeplitz = jnp.where(lag[None] >= 0, full, 0.0)
    signal = pencils.astype(jnp.float32).reshape(chan_here, blocks, block)
    precise = lax.Precision.HIGH
    inside = jnp.einsum("cnj,cjt->cnt", signal, toeplitz, precision=precise)
    to_end = jnp.exp(-(float(block - 1) - steps)[None, None, :] / life)
    leaving = jnp.einsum("cnj,rcj->rcn", signal, to_end, precision=precise)
    n_idx = jnp.arange(blocks, dtype=jnp.int32)
    gap = (n_idx[:, None] - 1 - n_idx[None, :]).astype(jnp.float32)
    exponent = jnp.where(
        (n_idx[:, None] > n_idx[None, :])[None, None],
        -float(block) * gap[None, None] / life[..., None],
        -jnp.inf,
    )
    entering = jnp.sum(jnp.exp(exponent) * leaving[:, :, None, :], axis=-1)
    from_start = resid * jnp.exp(-(steps + 1.0)[None, None, :] / life)
    carried = jnp.einsum("rcn,rct->cnt", entering, from_start, precision=precise)
    return (inside + carried).reshape(chan_here, length)


def project_kernel(core_ref, gated_ref, weight_ref, out_ref):
    out_ref[...] = jnp.dot(
        gated_ref[...], weight_ref[...], preferred_element_type=jnp.float32
    ).astype(out_ref.dtype)


def quarter_slot(quarter, core):
    differ = quarter % 2 - core
    return quarter // 2 + 2 * (1 - differ * differ)


def project_and_reduce(gated_rows, out_weight):
    chans, toks = gated_rows.shape
    outs = out_weight.shape[1]
    width = outs // 4
    index = lax.axis_index("chan")
    chip, core = index // 2, index % 2
    partial = pl.pallas_call(
        project_kernel,
        grid_spec=pltpu.PrefetchScalarGridSpec(
            num_scalar_prefetch=1,
            grid=(4,),
            in_specs=[
                pl.BlockSpec((toks, chans), lambda j, c: (0, 0)),
                pl.BlockSpec((chans, width), lambda j, c: (0, j)),
            ],
            out_specs=pl.BlockSpec((toks, width), lambda j, c: (0, quarter_slot(j, c[0]))),
        ),
        out_shape=jax.ShapeDtypeStruct((toks, outs), jnp.bfloat16),
    )(jnp.reshape(core, (1,)).astype(jnp.int32), gated_rows.T, out_weight)
    slot = [partial[:, q * width : (q + 1) * width] for q in range(4)]
    send = jnp.stack(slot[:2])
    keep = jnp.stack(slot[2:])
    got = lax.ppermute(send, "chan", [(j, j ^ 1) for j in range(4)])
    halves = keep.astype(jnp.float32) + got.astype(jnp.float32)
    first = chip == 0
    send2 = jnp.where(first, halves[1], halves[0]).astype(jnp.bfloat16)
    keep2 = jnp.where(first, halves[0], halves[1])
    got2 = lax.ppermute(send2, "chan", [(j, j ^ 2) for j in range(4)])
    return (keep2 + got2.astype(jnp.float32)).astype(jnp.bfloat16).T


def local(qkv, taps, lifetimes, residues, out_weight):
    chan_local = qkv.shape[1]
    tok_count = qkv.shape[2]
    edge_block = qkv[:, :, tok_count - 2 :]
    earlier = from_behind(edge_block, "seq", 1)
    extended = jnp.concatenate([earlier, qkv], axis=2).astype(jnp.float32)
    filtered = (
        taps[:, 0, :, None] * extended[:, :, 2:]
        + taps[:, 1, :, None] * extended[:, :, 1:-1]
        + taps[:, 2, :, None] * extended[:, :, :-2]
    )
    product = (filtered[1] * filtered[2]).astype(jnp.bfloat16)
    groups = lax.axis_size("seq")
    per_group = chan_local // groups
    pencils = lax.all_to_all(product, "seq", split_axis=0, concat_axis=1, tiled=True)
    first_chan = lax.axis_index("seq") * per_group
    life_slice = lax.dynamic_slice_in_dim(lifetimes, first_chan, per_group, 1)
    resid_slice = lax.dynamic_slice_in_dim(residues, first_chan, per_group, 1)
    convolved = modal_conv(pencils, life_slice, resid_slice).astype(jnp.bfloat16)
    returned = lax.all_to_all(convolved, "seq", split_axis=1, concat_axis=0, tiled=True)
    gated_rows = (filtered[0] * returned.astype(jnp.float32)).astype(jnp.bfloat16)
    return project_and_reduce(gated_rows, out_weight)


def solution(mesh):
    placed = (
        P(None, "chan", "seq"),
        P(None, None, "chan"),
        P(None, "chan"),
        P(None, "chan"),
        P("chan", None),
    )
    return jax.shard_map(
        local, mesh=mesh, in_specs=placed, out_specs=P("chan", "seq"), check_vma=False
    )
```

```python
import jax
import jax.numpy as jnp
from jax import lax
from jax.sharding import PartitionSpec as P


def from_behind(x, axis, by):
    devices = lax.axis_size(axis)
    pairs = [(i, i + by) for i in range(devices) if 0 <= i + by < devices]
    return lax.ppermute(x, axis, pairs)


def modal_conv(pencils, life_slice, resid_slice, block=128):
    chan_here, length = pencils.shape
    blocks = length // block
    steps = jnp.arange(block, dtype=jnp.int32).astype(jnp.float32)
    life = life_slice[:, :, None]
    resid = resid_slice[:, :, None]
    offs = steps - float(block // 2)
    rising = resid * jnp.exp(offs[None, None, :] / life)
    falling = jnp.exp(-offs[None, None, :] / life)
    full = jnp.einsum("rcj,rct->cjt", rising, falling, precision=lax.Precision.HIGHEST)
    lag = jnp.arange(block, dtype=jnp.int32)[None, :] - jnp.arange(block, dtype=jnp.int32)[:, None]
    toeplitz = jnp.where(lag[None] >= 0, full, 0.0)
    signal = pencils.astype(jnp.float32).reshape(chan_here, blocks, block)
    precise = lax.Precision.HIGH
    inside = jnp.einsum("cnj,cjt->cnt", signal, toeplitz, precision=precise)
    to_end = jnp.exp(-(float(block - 1) - steps)[None, None, :] / life)
    leaving = jnp.einsum("cnj,rcj->rcn", signal, to_end, precision=precise)
    n_idx = jnp.arange(blocks, dtype=jnp.int32)
    gap = (n_idx[:, None] - 1 - n_idx[None, :]).astype(jnp.float32)
    exponent = jnp.where(
        (n_idx[:, None] > n_idx[None, :])[None, None],
        -float(block) * gap[None, None] / life[..., None],
        -jnp.inf,
    )
    entering = jnp.sum(jnp.exp(exponent) * leaving[:, :, None, :], axis=-1)
    from_start = resid * jnp.exp(-(steps + 1.0)[None, None, :] / life)
    carried = jnp.einsum("rcn,rct->cnt", entering, from_start, precision=precise)
    return (inside + carried).reshape(chan_here, length)


def reduce_scatter_chan(partial):
    index = lax.axis_index("chan")
    chip, core = index // 2, index % 2
    width = partial.shape[1] // 4
    quarter = [partial[:, q * width : (q + 1) * width] for q in range(4)]
    mine = core == 0
    send = jnp.stack([jnp.where(mine, quarter[2 * h + 1], quarter[2 * h]) for h in range(2)])
    keep = jnp.stack([jnp.where(mine, quarter[2 * h], quarter[2 * h + 1]) for h in range(2)])
    got = lax.ppermute(send, "chan", [(j, j ^ 1) for j in range(4)])
    halves = keep.astype(jnp.float32) + got.astype(jnp.float32)
    first = chip == 0
    send2 = jnp.where(first, halves[1], halves[0]).astype(jnp.bfloat16)
    keep2 = jnp.where(first, halves[0], halves[1])
    got2 = lax.ppermute(send2, "chan", [(j, j ^ 2) for j in range(4)])
    return (keep2 + got2.astype(jnp.float32)).astype(jnp.bfloat16).T


def local(qkv, taps, lifetimes, residues, out_weight):
    chan_local = qkv.shape[1]
    tok_count = qkv.shape[2]
    edge_block = qkv[:, :, tok_count - 2 :]
    earlier = from_behind(edge_block, "seq", 1)

    signal = qkv.astype(jnp.float32)
    pad1 = jnp.zeros(signal.shape[:2] + (1,), jnp.float32)
    pad2 = jnp.zeros(signal.shape[:2] + (2,), jnp.float32)
    no_halo = (
        taps[:, 0, :, None] * signal
        + taps[:, 1, :, None] * jnp.concatenate([pad1, signal[:, :, :-1]], axis=2)
        + taps[:, 2, :, None] * jnp.concatenate([pad2, signal[:, :, :-2]], axis=2)
    )
    body, filtered_q = lax.optimization_barrier(
        ((no_halo[1] * no_halo[2]).astype(jnp.bfloat16), no_halo[0])
    )
    head_in = jnp.concatenate([earlier, qkv[:, :, :2]], axis=2).astype(jnp.float32)
    head = (
        taps[:, 0, :, None] * head_in[:, :, 2:]
        + taps[:, 1, :, None] * head_in[:, :, 1:3]
        + taps[:, 2, :, None] * head_in[:, :, :2]
    )
    product = lax.dynamic_update_slice(body, (head[1] * head[2]).astype(jnp.bfloat16), (0, 0))
    filtered_q = lax.dynamic_update_slice(filtered_q, head[0], (0, 0))
    groups = lax.axis_size("seq")
    per_group = chan_local // groups
    pencils = lax.all_to_all(product, "seq", split_axis=0, concat_axis=1, tiled=True)
    first_chan = lax.axis_index("seq") * per_group
    life_slice = lax.dynamic_slice_in_dim(lifetimes, first_chan, per_group, 1)
    resid_slice = lax.dynamic_slice_in_dim(residues, first_chan, per_group, 1)
    convolved = modal_conv(pencils, life_slice, resid_slice).astype(jnp.bfloat16)
    returned = lax.all_to_all(convolved, "seq", split_axis=1, concat_axis=0, tiled=True)
    gated_rows = (filtered_q * returned.astype(jnp.float32)).astype(jnp.bfloat16)
    partial = lax.dot_general(
        gated_rows, out_weight, (((0,), (0,)), ((), ())), preferred_element_type=jnp.float32
    ).astype(jnp.bfloat16)
    return reduce_scatter_chan(partial)


def solution(mesh):
    placed = (
        P(None, "chan", "seq"),
        P(None, None, "chan"),
        P(None, "chan"),
        P(None, "chan"),
        P("chan", None),
    )
    return jax.shard_map(
        local, mesh=mesh, in_specs=placed, out_specs=P("chan", "seq"), check_vma=False
    )
```

```python
import jax
import jax.numpy as jnp
from jax import lax
from jax.sharding import PartitionSpec as P


def from_behind(x, axis, by):
    devices = lax.axis_size(axis)
    pairs = [(i, i + by) for i in range(devices) if 0 <= i + by < devices]
    return lax.ppermute(x, axis, pairs)


def modal_conv(pencils, life_slice, resid_slice, block=256):
    chan_here, length = pencils.shape
    blocks = length // block
    steps = jnp.arange(block, dtype=jnp.int32).astype(jnp.float32)
    life = life_slice[:, :, None]
    resid = resid_slice[:, :, None]
    offs = steps - float(block // 2)
    rising = resid * jnp.exp(offs[None, None, :] / life)
    falling = jnp.exp(-offs[None, None, :] / life)
    full = jnp.einsum("rcj,rct->cjt", rising, falling, precision=lax.Precision.HIGHEST)
    lag = jnp.arange(block, dtype=jnp.int32)[None, :] - jnp.arange(block, dtype=jnp.int32)[:, None]
    toeplitz = jnp.where(lag[None] >= 0, full, 0.0)
    signal = pencils.astype(jnp.float32).reshape(chan_here, blocks, block)
    precise = lax.Precision.HIGH
    inside = jnp.einsum("cnj,cjt->cnt", signal, toeplitz, precision=precise)
    to_end = jnp.exp(-(float(block - 1) - steps)[None, None, :] / life)
    leaving = jnp.einsum("cnj,rcj->rcn", signal, to_end, precision=precise)
    n_idx = jnp.arange(blocks, dtype=jnp.int32)
    gap = (n_idx[:, None] - 1 - n_idx[None, :]).astype(jnp.float32)
    exponent = jnp.where(
        (n_idx[:, None] > n_idx[None, :])[None, None],
        -float(block) * gap[None, None] / life[..., None],
        -jnp.inf,
    )
    entering = jnp.sum(jnp.exp(exponent) * leaving[:, :, None, :], axis=-1)
    from_start = resid * jnp.exp(-(steps + 1.0)[None, None, :] / life)
    carried = jnp.einsum("rcn,rct->cnt", entering, from_start, precision=precise)
    return (inside + carried).reshape(chan_here, length)


def reduce_scatter_chan(partial):
    index = lax.axis_index("chan")
    chip, core = index // 2, index % 2
    width = partial.shape[1] // 4
    quarter = [partial[:, q * width : (q + 1) * width] for q in range(4)]
    mine = core == 0
    send = jnp.stack([jnp.where(mine, quarter[2 * h + 1], quarter[2 * h]) for h in range(2)])
    keep = jnp.stack([jnp.where(mine, quarter[2 * h], quarter[2 * h + 1]) for h in range(2)])
    got = lax.ppermute(send, "chan", [(j, j ^ 1) for j in range(4)])
    halves = keep.astype(jnp.float32) + got.astype(jnp.float32)
    first = chip == 0
    send2 = jnp.where(first, halves[1], halves[0]).astype(jnp.bfloat16)
    keep2 = jnp.where(first, halves[0], halves[1])
    got2 = lax.ppermute(send2, "chan", [(j, j ^ 2) for j in range(4)])
    return (keep2 + got2.astype(jnp.float32)).astype(jnp.bfloat16).T


def local(qkv, taps, lifetimes, residues, out_weight):
    chan_local = qkv.shape[1]
    tok_count = qkv.shape[2]
    edge_block = qkv[:, :, tok_count - 2 :]
    earlier = from_behind(edge_block, "seq", 1)
    extended = jnp.concatenate([earlier, qkv], axis=2).astype(jnp.float32)
    filtered = (
        taps[:, 0, :, None] * extended[:, :, 2:]
        + taps[:, 1, :, None] * extended[:, :, 1:-1]
        + taps[:, 2, :, None] * extended[:, :, :-2]
    )
    product = (filtered[1] * filtered[2]).astype(jnp.bfloat16)
    groups = lax.axis_size("seq")
    per_group = chan_local // groups
    pencils = lax.all_to_all(product, "seq", split_axis=0, concat_axis=1, tiled=True)
    first_chan = lax.axis_index("seq") * per_group
    life_slice = lax.dynamic_slice_in_dim(lifetimes, first_chan, per_group, 1)
    resid_slice = lax.dynamic_slice_in_dim(residues, first_chan, per_group, 1)
    convolved = modal_conv(pencils, life_slice, resid_slice).astype(jnp.bfloat16)
    returned = lax.all_to_all(convolved, "seq", split_axis=1, concat_axis=0, tiled=True)
    gated_rows = (filtered[0] * returned.astype(jnp.float32)).astype(jnp.bfloat16)
    partial = lax.dot_general(
        gated_rows, out_weight, (((0,), (0,)), ((), ())), preferred_element_type=jnp.float32
    ).astype(jnp.bfloat16)
    return reduce_scatter_chan(partial)


def solution(mesh):
    placed = (
        P(None, "chan", "seq"),
        P(None, None, "chan"),
        P(None, "chan"),
        P(None, "chan"),
        P("chan", None),
    )
    return jax.shard_map(
        local, mesh=mesh, in_specs=placed, out_specs=P("chan", "seq"), check_vma=False
    )
```

```python
import jax
import jax.numpy as jnp
from jax import lax
from jax.sharding import PartitionSpec as P


def from_behind(x, axis, by):
    devices = lax.axis_size(axis)
    pairs = [(i, i + by) for i in range(devices) if 0 <= i + by < devices]
    return lax.ppermute(x, axis, pairs)


def modal_conv(pencils, life_slice, resid_slice, block=128):
    chan_here, length = pencils.shape
    blocks = length // block
    steps = jnp.arange(block, dtype=jnp.int32).astype(jnp.float32)
    life = life_slice[:, :, None]
    resid = resid_slice[:, :, None]
    offs = steps - float(block // 2)
    rising = resid * jnp.exp(offs[None, None, :] / life)
    falling = jnp.exp(-offs[None, None, :] / life)
    full = jnp.einsum("rcj,rct->cjt", rising, falling, precision=lax.Precision.HIGHEST)
    lag = jnp.arange(block, dtype=jnp.int32)[None, :] - jnp.arange(block, dtype=jnp.int32)[:, None]
    toeplitz = jnp.where(lag[None] >= 0, full, 0.0)
    signal = pencils.astype(jnp.float32).reshape(chan_here, blocks, block)
    precise = lax.Precision.HIGH
    inside = jnp.einsum("cnj,cjt->cnt", signal, toeplitz, precision=precise)
    to_end = jnp.exp(-(float(block - 1) - steps)[None, None, :] / life)
    leaving = jnp.einsum("cnj,rcj->rcn", signal, to_end, precision=precise)
    n_idx = jnp.arange(blocks, dtype=jnp.int32)
    gap = (n_idx[:, None] - 1 - n_idx[None, :]).astype(jnp.float32)
    exponent = jnp.where(
        (n_idx[:, None] > n_idx[None, :])[None, None],
        -float(block) * gap[None, None] / life[..., None],
        -jnp.inf,
    )
    decays = lax.optimization_barrier(jnp.exp(exponent))
    entering = jnp.sum(decays * leaving[:, :, None, :], axis=-1)
    from_start = resid * jnp.exp(-(steps + 1.0)[None, None, :] / life)
    carried = jnp.einsum("rcn,rct->cnt", entering, from_start, precision=precise)
    return (inside + carried).reshape(chan_here, length)


def reduce_scatter_chan(partial):
    index = lax.axis_index("chan")
    chip, core = index // 2, index % 2
    width = partial.shape[1] // 4
    quarter = [partial[:, q * width : (q + 1) * width] for q in range(4)]
    mine = core == 0
    send = jnp.stack([jnp.where(mine, quarter[2 * h + 1], quarter[2 * h]) for h in range(2)])
    keep = jnp.stack([jnp.where(mine, quarter[2 * h], quarter[2 * h + 1]) for h in range(2)])
    got = lax.ppermute(send, "chan", [(j, j ^ 1) for j in range(4)])
    halves = keep.astype(jnp.float32) + got.astype(jnp.float32)
    first = chip == 0
    send2 = jnp.where(first, halves[1], halves[0]).astype(jnp.bfloat16)
    keep2 = jnp.where(first, halves[0], halves[1])
    got2 = lax.ppermute(send2, "chan", [(j, j ^ 2) for j in range(4)])
    return (keep2 + got2.astype(jnp.float32)).astype(jnp.bfloat16).T


def local(qkv, taps, lifetimes, residues, out_weight):
    chan_local = qkv.shape[1]
    tok_count = qkv.shape[2]
    edge_block = qkv[:, :, tok_count - 2 :]
    earlier = from_behind(edge_block, "seq", 1)
    extended = jnp.concatenate([earlier, qkv], axis=2).astype(jnp.float32)
    filtered = (
        taps[:, 0, :, None] * extended[:, :, 2:]
        + taps[:, 1, :, None] * extended[:, :, 1:-1]
        + taps[:, 2, :, None] * extended[:, :, :-2]
    )
    product = (filtered[1] * filtered[2]).astype(jnp.bfloat16)
    groups = lax.axis_size("seq")
    per_group = chan_local // groups
    pencils = lax.all_to_all(product, "seq", split_axis=0, concat_axis=1, tiled=True)
    first_chan = lax.axis_index("seq") * per_group
    life_slice = lax.dynamic_slice_in_dim(lifetimes, first_chan, per_group, 1)
    resid_slice = lax.dynamic_slice_in_dim(residues, first_chan, per_group, 1)
    convolved = modal_conv(pencils, life_slice, resid_slice).astype(jnp.bfloat16)
    returned = lax.all_to_all(convolved, "seq", split_axis=1, concat_axis=0, tiled=True)
    gated_rows = (filtered[0] * returned.astype(jnp.float32)).astype(jnp.bfloat16)
    partial = lax.dot_general(
        gated_rows, out_weight, (((0,), (0,)), ((), ())), preferred_element_type=jnp.float32
    ).astype(jnp.bfloat16)
    return reduce_scatter_chan(partial)


def solution(mesh):
    placed = (
        P(None, "chan", "seq"),
        P(None, None, "chan"),
        P(None, "chan"),
        P(None, "chan"),
        P("chan", None),
    )
    return jax.shard_map(
        local, mesh=mesh, in_specs=placed, out_specs=P("chan", "seq"), check_vma=False
    )
```

```python
import jax
import jax.numpy as jnp
from jax import lax
from jax.sharding import PartitionSpec as P


def from_behind(x, axis, by):
    devices = lax.axis_size(axis)
    pairs = [(i, i + by) for i in range(devices) if 0 <= i + by < devices]
    return lax.ppermute(x, axis, pairs)


def modal_conv(pencils, life_slice, resid_slice, block=128):
    chan_here, length = pencils.shape
    blocks = length // block
    steps = jnp.arange(block, dtype=jnp.int32).astype(jnp.float32)
    life = life_slice[:, :, None]
    resid = resid_slice[:, :, None]
    offs = steps - float(block // 2)
    rising = resid * jnp.exp(offs[None, None, :] / life)
    falling = jnp.exp(-offs[None, None, :] / life)
    full = jnp.einsum("rcj,rct->cjt", rising, falling, precision=lax.Precision.HIGHEST)
    lag = jnp.arange(block, dtype=jnp.int32)[None, :] - jnp.arange(block, dtype=jnp.int32)[:, None]
    toeplitz = jnp.where(lag[None] >= 0, full, 0.0)
    signal = pencils.astype(jnp.float32).reshape(chan_here, blocks, block)
    precise = lax.Precision.HIGH
    inside = jnp.einsum("cnj,cjt->cnt", signal, toeplitz, precision=precise)
    to_end = jnp.exp(-(float(block - 1) - steps)[None, None, :] / life)
    leaving = jnp.einsum("cnj,rcj->rcn", signal, to_end, precision=precise)
    n_idx = jnp.arange(blocks, dtype=jnp.int32)
    gap = (n_idx[:, None] - 1 - n_idx[None, :]).astype(jnp.float32)
    exponent = jnp.where(
        (n_idx[:, None] > n_idx[None, :])[None, None],
        -float(block) * gap[None, None] / life[..., None],
        -jnp.inf,
    )
    entering = jnp.sum(jnp.exp(exponent) * leaving[:, :, None, :], axis=-1)
    from_start = resid * jnp.exp(-(steps + 1.0)[None, None, :] / life)
    carried = jnp.einsum("rcn,rct->cnt", entering, from_start, precision=precise)
    return (inside + carried).reshape(chan_here, length)


def reduce_scatter_chan(partial):
    index = lax.axis_index("chan")
    chip, core = index // 2, index % 2
    width = partial.shape[1] // 4
    quarter = [partial[:, q * width : (q + 1) * width] for q in range(4)]
    mine = core == 0
    send = jnp.stack([jnp.where(mine, quarter[2 * h + 1], quarter[2 * h]) for h in range(2)])
    keep = jnp.stack([jnp.where(mine, quarter[2 * h], quarter[2 * h + 1]) for h in range(2)])
    got = lax.ppermute(send, "chan", [(j, j ^ 1) for j in range(4)])
    halves = keep.astype(jnp.float32) + got.astype(jnp.float32)
    first = chip == 0
    send2 = jnp.where(first, halves[1], halves[0]).astype(jnp.bfloat16)
    keep2 = jnp.where(first, halves[0], halves[1])
    got2 = lax.ppermute(send2, "chan", [(j, j ^ 2) for j in range(4)])
    return (keep2 + got2.astype(jnp.float32)).astype(jnp.bfloat16).T


def local(qkv, taps, lifetimes, residues, out_weight):
    chan_local = qkv.shape[1]
    tok_count = qkv.shape[2]
    edge_block = qkv[:, :, tok_count - 2 :]
    devices = lax.axis_size("seq")
    wrapped = lax.ppermute(edge_block, "seq", [(i, (i + 1) % devices) for i in range(devices)])
    earlier = jnp.where(lax.axis_index("seq") == 0, jnp.zeros_like(wrapped), wrapped)
    extended = jnp.concatenate([earlier, qkv], axis=2).astype(jnp.float32)
    filtered = (
        taps[:, 0, :, None] * extended[:, :, 2:]
        + taps[:, 1, :, None] * extended[:, :, 1:-1]
        + taps[:, 2, :, None] * extended[:, :, :-2]
    )
    product = (filtered[1] * filtered[2]).astype(jnp.bfloat16)
    groups = lax.axis_size("seq")
    per_group = chan_local // groups
    pencils = lax.all_to_all(product, "seq", split_axis=0, concat_axis=1, tiled=True)
    first_chan = lax.axis_index("seq") * per_group
    life_slice = lax.dynamic_slice_in_dim(lifetimes, first_chan, per_group, 1)
    resid_slice = lax.dynamic_slice_in_dim(residues, first_chan, per_group, 1)
    convolved = modal_conv(pencils, life_slice, resid_slice).astype(jnp.bfloat16)
    returned = lax.all_to_all(convolved, "seq", split_axis=1, concat_axis=0, tiled=True)
    gated_rows = (filtered[0] * returned.astype(jnp.float32)).astype(jnp.bfloat16)
    partial = lax.dot_general(
        gated_rows, out_weight, (((0,), (0,)), ((), ())), preferred_element_type=jnp.float32
    ).astype(jnp.bfloat16)
    return reduce_scatter_chan(partial)


def solution(mesh):
    placed = (
        P(None, "chan", "seq"),
        P(None, None, "chan"),
        P(None, "chan"),
        P(None, "chan"),
        P("chan", None),
    )
    return jax.shard_map(
        local, mesh=mesh, in_specs=placed, out_specs=P("chan", "seq"), check_vma=False
    )
```

```python
import jax
import jax.numpy as jnp
from jax import lax
from jax.sharding import PartitionSpec as P


def from_behind(x, axis, by):
    devices = lax.axis_size(axis)
    pairs = [(i, i + by) for i in range(devices) if 0 <= i + by < devices]
    return lax.ppermute(x, axis, pairs)


def modal_conv(pencils, life_slice, resid_slice, block=128):
    chan_here, length = pencils.shape
    blocks = length // block
    steps = jnp.arange(block, dtype=jnp.int32).astype(jnp.float32)
    life = life_slice[:, :, None]
    resid = resid_slice[:, :, None]
    offs = steps - float(block // 2)
    rising = resid * jnp.exp(offs[None, None, :] / life)
    falling = jnp.exp(-offs[None, None, :] / life)
    full = jnp.einsum("rcj,rct->cjt", rising, falling, precision=lax.Precision.HIGHEST)
    lag = jnp.arange(block, dtype=jnp.int32)[None, :] - jnp.arange(block, dtype=jnp.int32)[:, None]
    toeplitz = jnp.where(lag[None] >= 0, full, 0.0)
    signal = pencils.astype(jnp.float32).reshape(chan_here, blocks, block)
    precise = lax.Precision.HIGH
    inside = jnp.einsum("cnj,cjt->cnt", signal, toeplitz, precision=precise)
    to_end = jnp.exp(-(float(block - 1) - steps)[None, None, :] / life)
    leaving = jnp.einsum("cnj,rcj->rcn", signal, to_end, precision=precise)
    gaps = jnp.arange(blocks - 1, dtype=jnp.int32).astype(jnp.float32)
    decay = jnp.exp(-float(block) * gaps[None, None, :] / life)
    padded = jnp.concatenate([jnp.zeros_like(leaving), leaving], axis=-1)
    entering = jnp.zeros_like(leaving)
    for k in range(blocks - 1):
        start = blocks - 1 - k
        entering = entering + decay[..., k : k + 1] * padded[..., start : start + blocks]
    from_start = resid * jnp.exp(-(steps + 1.0)[None, None, :] / life)
    carried = jnp.einsum("rcn,rct->cnt", entering, from_start, precision=precise)
    return (inside + carried).reshape(chan_here, length)


def reduce_scatter_chan(partial):
    index = lax.axis_index("chan")
    chip, core = index // 2, index % 2
    width = partial.shape[1] // 4
    quarter = [partial[:, q * width : (q + 1) * width] for q in range(4)]
    mine = core == 0
    send = jnp.stack([jnp.where(mine, quarter[2 * h + 1], quarter[2 * h]) for h in range(2)])
    keep = jnp.stack([jnp.where(mine, quarter[2 * h], quarter[2 * h + 1]) for h in range(2)])
    got = lax.ppermute(send, "chan", [(j, j ^ 1) for j in range(4)])
    halves = keep.astype(jnp.float32) + got.astype(jnp.float32)
    first = chip == 0
    send2 = jnp.where(first, halves[1], halves[0]).astype(jnp.bfloat16)
    keep2 = jnp.where(first, halves[0], halves[1])
    got2 = lax.ppermute(send2, "chan", [(j, j ^ 2) for j in range(4)])
    return (keep2 + got2.astype(jnp.float32)).astype(jnp.bfloat16).T


def local(qkv, taps, lifetimes, residues, out_weight):
    chan_local = qkv.shape[1]
    tok_count = qkv.shape[2]
    edge_block = qkv[:, :, tok_count - 2 :]
    devices = lax.axis_size("seq")
    wrapped = lax.ppermute(edge_block, "seq", [(i, (i + 1) % devices) for i in range(devices)])
    earlier = jnp.where(lax.axis_index("seq") == 0, jnp.zeros_like(wrapped), wrapped)
    extended = jnp.concatenate([earlier, qkv], axis=2).astype(jnp.float32)
    filtered = (
        taps[:, 0, :, None] * extended[:, :, 2:]
        + taps[:, 1, :, None] * extended[:, :, 1:-1]
        + taps[:, 2, :, None] * extended[:, :, :-2]
    )
    product = (filtered[1] * filtered[2]).astype(jnp.bfloat16)
    groups = lax.axis_size("seq")
    per_group = chan_local // groups
    pencils = lax.all_to_all(product, "seq", split_axis=0, concat_axis=1, tiled=True)
    first_chan = lax.axis_index("seq") * per_group
    life_slice = lax.dynamic_slice_in_dim(lifetimes, first_chan, per_group, 1)
    resid_slice = lax.dynamic_slice_in_dim(residues, first_chan, per_group, 1)
    convolved = modal_conv(pencils, life_slice, resid_slice).astype(jnp.bfloat16)
    returned = lax.all_to_all(convolved, "seq", split_axis=1, concat_axis=0, tiled=True)
    gated_rows = (filtered[0] * returned.astype(jnp.float32)).astype(jnp.bfloat16)
    partial = lax.dot_general(
        gated_rows, out_weight, (((0,), (0,)), ((), ())), preferred_element_type=jnp.float32
    ).astype(jnp.bfloat16)
    return reduce_scatter_chan(partial)


def solution(mesh):
    placed = (
        P(None, "chan", "seq"),
        P(None, None, "chan"),
        P(None, "chan"),
        P(None, "chan"),
        P("chan", None),
    )
    return jax.shard_map(
        local, mesh=mesh, in_specs=placed, out_specs=P("chan", "seq"), check_vma=False
    )
```

```python
import jax
import jax.numpy as jnp
from jax import lax
from jax.sharding import PartitionSpec as P


def from_behind(x, axis, by):
    devices = lax.axis_size(axis)
    pairs = [(i, i + by) for i in range(devices) if 0 <= i + by < devices]
    return lax.ppermute(x, axis, pairs)


def modal_conv(pencils, life_slice, resid_slice, block=128):
    chan_here, length = pencils.shape
    blocks = length // block
    steps = jnp.arange(block, dtype=jnp.int32).astype(jnp.float32)
    life = life_slice[:, :, None]
    resid = resid_slice[:, :, None]
    offs = steps - float(block // 2)
    rising = resid * jnp.exp(offs[None, None, :] / life)
    falling = jnp.exp(-offs[None, None, :] / life)
    full = jnp.einsum("rcj,rct->cjt", rising, falling, precision=lax.Precision.HIGHEST)
    lag = jnp.arange(block, dtype=jnp.int32)[None, :] - jnp.arange(block, dtype=jnp.int32)[:, None]
    toeplitz = jnp.where(lag[None] >= 0, full, 0.0)
    signal = pencils.astype(jnp.float32).reshape(chan_here, blocks, block)
    precise = lax.Precision.HIGH
    inside = jnp.einsum("cnj,cjt->cnt", signal, toeplitz, precision=precise)
    to_end = jnp.exp(-(float(block - 1) - steps)[None, None, :] / life)
    leaving = jnp.einsum("cnj,rcj->rcn", signal, to_end, precision=precise)
    n_idx = jnp.arange(blocks, dtype=jnp.int32)
    gap = (n_idx[:, None] - 1 - n_idx[None, :]).astype(jnp.float32)
    exponent = jnp.where(
        (n_idx[:, None] > n_idx[None, :])[None, None],
        -float(block) * gap[None, None] / life[..., None],
        -jnp.inf,
    )
    entering = jnp.einsum(
        "rcnm,rcm->rcn", jnp.exp(exponent), leaving, precision=lax.Precision.HIGHEST
    )
    from_start = resid * jnp.exp(-(steps + 1.0)[None, None, :] / life)
    carried = jnp.einsum("rcn,rct->cnt", entering, from_start, precision=precise)
    return (inside + carried).reshape(chan_here, length)


def reduce_scatter_chan(partial):
    index = lax.axis_index("chan")
    chip, core = index // 2, index % 2
    width = partial.shape[1] // 4
    quarter = [partial[:, q * width : (q + 1) * width] for q in range(4)]
    mine = core == 0
    send = jnp.stack([jnp.where(mine, quarter[2 * h + 1], quarter[2 * h]) for h in range(2)])
    keep = jnp.stack([jnp.where(mine, quarter[2 * h], quarter[2 * h + 1]) for h in range(2)])
    got = lax.ppermute(send, "chan", [(j, j ^ 1) for j in range(4)])
    halves = keep.astype(jnp.float32) + got.astype(jnp.float32)
    first = chip == 0
    send2 = jnp.where(first, halves[1], halves[0]).astype(jnp.bfloat16)
    keep2 = jnp.where(first, halves[0], halves[1])
    got2 = lax.ppermute(send2, "chan", [(j, j ^ 2) for j in range(4)])
    return (keep2 + got2.astype(jnp.float32)).astype(jnp.bfloat16).T


def local(qkv, taps, lifetimes, residues, out_weight):
    chan_local = qkv.shape[1]
    tok_count = qkv.shape[2]
    edge_block = qkv[:, :, tok_count - 2 :]
    devices = lax.axis_size("seq")
    wrapped = lax.ppermute(edge_block, "seq", [(i, (i + 1) % devices) for i in range(devices)])
    earlier = jnp.where(lax.axis_index("seq") == 0, jnp.zeros_like(wrapped), wrapped)
    extended = jnp.concatenate([earlier, qkv], axis=2).astype(jnp.float32)
    filtered = (
        taps[:, 0, :, None] * extended[:, :, 2:]
        + taps[:, 1, :, None] * extended[:, :, 1:-1]
        + taps[:, 2, :, None] * extended[:, :, :-2]
    )
    product = (filtered[1] * filtered[2]).astype(jnp.bfloat16)
    groups = lax.axis_size("seq")
    per_group = chan_local // groups
    pencils = lax.all_to_all(product, "seq", split_axis=0, concat_axis=1, tiled=True)
    first_chan = lax.axis_index("seq") * per_group
    life_slice = lax.dynamic_slice_in_dim(lifetimes, first_chan, per_group, 1)
    resid_slice = lax.dynamic_slice_in_dim(residues, first_chan, per_group, 1)
    convolved = modal_conv(pencils, life_slice, resid_slice).astype(jnp.bfloat16)
    returned = lax.all_to_all(convolved, "seq", split_axis=1, concat_axis=0, tiled=True)
    gated_rows = (filtered[0] * returned.astype(jnp.float32)).astype(jnp.bfloat16)
    partial = lax.dot_general(
        gated_rows, out_weight, (((0,), (0,)), ((), ())), preferred_element_type=jnp.float32
    ).astype(jnp.bfloat16)
    return reduce_scatter_chan(partial)


def solution(mesh):
    placed = (
        P(None, "chan", "seq"),
        P(None, None, "chan"),
        P(None, "chan"),
        P(None, "chan"),
        P("chan", None),
    )
    return jax.shard_map(
        local, mesh=mesh, in_specs=placed, out_specs=P("chan", "seq"), check_vma=False
    )
```

```python
import jax
import jax.numpy as jnp
from jax import lax
from jax.sharding import PartitionSpec as P


def from_behind(x, axis, by):
    devices = lax.axis_size(axis)
    pairs = [(i, i + by) for i in range(devices) if 0 <= i + by < devices]
    return lax.ppermute(x, axis, pairs)


def modal_conv(pencils, life_slice, resid_slice, block=128):
    chan_here, length = pencils.shape
    blocks = length // block
    steps = jnp.arange(block, dtype=jnp.int32).astype(jnp.float32)
    life = life_slice[:, :, None]
    resid = resid_slice[:, :, None]
    offs = steps - float(block // 2)
    rising = resid * jnp.exp(offs[None, None, :] / life)
    falling = jnp.exp(-offs[None, None, :] / life)
    full = jnp.einsum("rcj,rct->cjt", rising, falling, precision=lax.Precision.HIGHEST)
    lag = jnp.arange(block, dtype=jnp.int32)[None, :] - jnp.arange(block, dtype=jnp.int32)[:, None]
    toeplitz = jnp.where(lag[None] >= 0, full, 0.0)
    signal = pencils.astype(jnp.float32).reshape(chan_here, blocks, block)
    precise = lax.Precision.HIGH
    inside = jnp.einsum("cnj,cjt->cnt", signal, toeplitz, precision=precise)
    to_end = jnp.exp(-(float(block - 1) - steps)[None, None, :] / life)
    leaving = jnp.einsum("cnj,rcj->rcn", signal, to_end, precision=precise)
    n_idx = jnp.arange(blocks, dtype=jnp.int32)
    gap = (n_idx[:, None] - 1 - n_idx[None, :]).astype(jnp.float32)
    exponent = jnp.where(
        (n_idx[:, None] > n_idx[None, :])[None, None],
        -float(block) * gap[None, None] / life[..., None],
        -jnp.inf,
    )
    entering = jnp.sum(jnp.exp(exponent) * leaving[:, :, None, :], axis=-1)
    from_start = resid * jnp.exp(-(steps + 1.0)[None, None, :] / life)
    carried = jnp.einsum("rcn,rct->cnt", entering, from_start, precision=precise)
    return (inside + carried).reshape(chan_here, length)


def reduce_scatter_chan(partial):
    index = lax.axis_index("chan")
    chip, core = index // 2, index % 2
    width = partial.shape[1] // 4
    quarter = [partial[:, q * width : (q + 1) * width] for q in range(4)]
    mine = core == 0
    send = jnp.stack([jnp.where(mine, quarter[2 * h + 1], quarter[2 * h]) for h in range(2)])
    keep = jnp.stack([jnp.where(mine, quarter[2 * h], quarter[2 * h + 1]) for h in range(2)])
    got = lax.ppermute(send, "chan", [(j, j ^ 1) for j in range(4)])
    halves = keep.astype(jnp.float32) + got.astype(jnp.float32)
    first = chip == 0
    send2 = jnp.where(first, halves[1], halves[0]).astype(jnp.bfloat16)
    keep2 = jnp.where(first, halves[0], halves[1])
    got2 = lax.ppermute(send2, "chan", [(j, j ^ 2) for j in range(4)])
    return (keep2 + got2.astype(jnp.float32)).astype(jnp.bfloat16).T


def local(qkv, taps, lifetimes, residues, out_weight):
    chan_local = qkv.shape[1]
    tok_count = qkv.shape[2]
    edge_block = qkv[:, :, tok_count - 2 :]
    devices = lax.axis_size("seq")
    wrapped = lax.ppermute(edge_block, "seq", [(i, (i + 1) % devices) for i in range(devices)])
    earlier = jnp.where(lax.axis_index("seq") == 0, jnp.zeros_like(wrapped), wrapped)
    extended = jnp.concatenate([earlier, qkv], axis=2).astype(jnp.float32)

    def filtered(stream):
        return (
            taps[stream, 0, :, None] * extended[stream, :, 2:]
            + taps[stream, 1, :, None] * extended[stream, :, 1:-1]
            + taps[stream, 2, :, None] * extended[stream, :, :-2]
        )

    product = (filtered(1) * filtered(2)).astype(jnp.bfloat16)
    groups = lax.axis_size("seq")
    per_group = chan_local // groups
    pencils = lax.all_to_all(product, "seq", split_axis=0, concat_axis=1, tiled=True)
    first_chan = lax.axis_index("seq") * per_group
    life_slice = lax.dynamic_slice_in_dim(lifetimes, first_chan, per_group, 1)
    resid_slice = lax.dynamic_slice_in_dim(residues, first_chan, per_group, 1)
    convolved = modal_conv(pencils, life_slice, resid_slice).astype(jnp.bfloat16)
    returned = lax.all_to_all(convolved, "seq", split_axis=1, concat_axis=0, tiled=True)
    gated_rows = (filtered(0) * returned.astype(jnp.float32)).astype(jnp.bfloat16)
    partial = lax.dot_general(
        gated_rows, out_weight, (((0,), (0,)), ((), ())), preferred_element_type=jnp.float32
    ).astype(jnp.bfloat16)
    return reduce_scatter_chan(partial)


def solution(mesh):
    placed = (
        P(None, "chan", "seq"),
        P(None, None, "chan"),
        P(None, "chan"),
        P(None, "chan"),
        P("chan", None),
    )
    return jax.shard_map(
        local, mesh=mesh, in_specs=placed, out_specs=P("chan", "seq"), check_vma=False
    )
```

```python
import jax
import jax.numpy as jnp
from jax import lax
from jax.sharding import PartitionSpec as P


def from_behind(x, axis, by):
    devices = lax.axis_size(axis)
    pairs = [(i, i + by) for i in range(devices) if 0 <= i + by < devices]
    return lax.ppermute(x, axis, pairs)


def modal_conv(pencils, life_slice, resid_slice, block=128):
    chan_here, length = pencils.shape
    blocks = length // block
    steps = jnp.arange(block, dtype=jnp.int32).astype(jnp.float32)
    life = life_slice[:, :, None]
    resid = resid_slice[:, :, None]
    offs = steps - float(block // 2)
    rising = resid * jnp.exp(offs[None, None, :] / life)
    falling = jnp.exp(-offs[None, None, :] / life)
    full = jnp.einsum("rcj,rct->cjt", rising, falling, precision=lax.Precision.HIGHEST)
    lag = jnp.arange(block, dtype=jnp.int32)[None, :] - jnp.arange(block, dtype=jnp.int32)[:, None]
    toeplitz = jnp.where(lag[None] >= 0, full, 0.0)
    signal = pencils.astype(jnp.float32).reshape(chan_here, blocks, block)
    precise = lax.Precision.HIGH
    inside = jnp.einsum("cnj,cjt->cnt", signal, toeplitz, precision=precise)
    to_end = jnp.exp(-(float(block - 1) - steps)[None, None, :] / life)
    leaving = jnp.einsum("cnj,rcj->rcn", signal, to_end, precision=precise)
    n_idx = jnp.arange(blocks, dtype=jnp.int32)
    gap = (n_idx[:, None] - 1 - n_idx[None, :]).astype(jnp.float32)
    exponent = jnp.where(
        (n_idx[:, None] > n_idx[None, :])[None, None],
        -float(block) * gap[None, None] / life[..., None],
        -jnp.inf,
    )
    entering = jnp.sum(jnp.exp(exponent) * leaving[:, :, None, :], axis=-1)
    from_start = resid * jnp.exp(-(steps + 1.0)[None, None, :] / life)
    carried = jnp.einsum("rcn,rct->cnt", entering, from_start, precision=precise)
    return (inside + carried).reshape(chan_here, length)


def reduce_scatter_chan(partial):
    index = lax.axis_index("chan")
    chip, core = index // 2, index % 2
    width = partial.shape[1] // 4
    quarter = [partial[:, q * width : (q + 1) * width] for q in range(4)]
    mine = core == 0
    send = jnp.stack([jnp.where(mine, quarter[2 * h + 1], quarter[2 * h]) for h in range(2)])
    keep = jnp.stack([jnp.where(mine, quarter[2 * h], quarter[2 * h + 1]) for h in range(2)])
    got = lax.ppermute(send, "chan", [(j, j ^ 1) for j in range(4)])
    halves = keep.astype(jnp.float32) + got.astype(jnp.float32)
    first = chip == 0
    send2 = jnp.where(first, halves[1], halves[0]).astype(jnp.bfloat16)
    keep2 = jnp.where(first, halves[0], halves[1])
    got2 = lax.ppermute(send2, "chan", [(j, j ^ 2) for j in range(4)])
    return (keep2 + got2.astype(jnp.float32)).astype(jnp.bfloat16).T


def local(qkv, taps, lifetimes, residues, out_weight):
    chan_local = qkv.shape[1]
    tok_count = qkv.shape[2]
    devices = lax.axis_size("seq")
    first_seq = lax.axis_index("seq") == 0

    def halo(block):
        wrapped = lax.ppermute(block, "seq", [(i, (i + 1) % devices) for i in range(devices)])
        return jnp.where(first_seq, jnp.zeros_like(wrapped), wrapped)

    def short_filter(stream_x, stream_taps, earlier):
        extended = jnp.concatenate([earlier, stream_x], axis=-1).astype(jnp.float32)
        return (
            stream_taps[..., 0, :, None] * extended[..., 2:]
            + stream_taps[..., 1, :, None] * extended[..., 1:-1]
            + stream_taps[..., 2, :, None] * extended[..., :-2]
        )

    kv_filtered = short_filter(qkv[1:], taps[1:], halo(qkv[1:, :, tok_count - 2 :]))
    product = (kv_filtered[0] * kv_filtered[1]).astype(jnp.bfloat16)
    q_earlier = halo(qkv[0, :, tok_count - 2 :])
    groups = lax.axis_size("seq")
    per_group = chan_local // groups
    pencils = lax.all_to_all(product, "seq", split_axis=0, concat_axis=1, tiled=True)
    first_chan = lax.axis_index("seq") * per_group
    life_slice = lax.dynamic_slice_in_dim(lifetimes, first_chan, per_group, 1)
    resid_slice = lax.dynamic_slice_in_dim(residues, first_chan, per_group, 1)
    convolved = modal_conv(pencils, life_slice, resid_slice).astype(jnp.bfloat16)
    returned = lax.all_to_all(convolved, "seq", split_axis=1, concat_axis=0, tiled=True)
    gated_rows = (short_filter(qkv[0], taps[0], q_earlier) * returned.astype(jnp.float32)).astype(jnp.bfloat16)
    partial = lax.dot_general(
        gated_rows, out_weight, (((0,), (0,)), ((), ())), preferred_element_type=jnp.float32
    ).astype(jnp.bfloat16)
    return reduce_scatter_chan(partial)


def solution(mesh):
    placed = (
        P(None, "chan", "seq"),
        P(None, None, "chan"),
        P(None, "chan"),
        P(None, "chan"),
        P("chan", None),
    )
    return jax.shard_map(
        local, mesh=mesh, in_specs=placed, out_specs=P("chan", "seq"), check_vma=False
    )
```
